128 devices in a mesh: ctx: 4 (over x_hi, core), exp: 32 (over z, y, x_lo).
Axes of the slice: x: 4 (x_hi: 2, x_lo: 2; x = x_hi * 2 + x_lo), y: 4, z: 4, core: 2. Of those that a mesh axis runs over, the one named last changes fastest.
Arguments:
- queries: bfloat16 [4096, 8192], P('ctx', 'exp'), may hold values from -32 to 32
- keys: bfloat16 [4096, 8192], P('ctx', 'exp'), may hold values from -4 to 4
- values: bfloat16 [4096, 8192], P('ctx', 'exp'), may hold values from -6 to 6
- out_proj: bfloat16 [8192, 3584], P('exp'), may hold values from -0.5 to 0.5
- residual: bfloat16 [4096, 3584], P(('ctx', 'exp')), may hold values from -6 to 6
- norm_gain: float32 [3584], replicated, may hold values from 0.25 to 1.75
- routes: int32 [4096, 8], P(('ctx', 'exp')), may hold values from 0 to 31, all different within a row; in each aligned block of 32 rows (0 to 31, 32 to 63, ...) at most 10 rows name the same one
- combine: float32 [4096, 8], P(('ctx', 'exp')), may hold values from 0.1 to 0.5
- w_gate: bfloat16 [32, 3584, 1024], P('exp', None, 'ctx'), may hold values from -0.09375 to 0.09375
- w_up: bfloat16 [32, 3584, 1024], P('exp', None, 'ctx'), may hold values from -0.09375 to 0.09375
- w_down: bfloat16 [32, 1024, 3584], P('exp', 'ctx'), may hold values from -0.1875 to 0.1875
Outputs:
- layer_out: bfloat16 [4096, 3584], P(('ctx', 'exp'))
The draws below stay inside these ranges and needn't reach their ends.
Inputs may be any that keep to these rules, and one draw needn't show every extreme that they name: `routes`: each row names 8 different experts. Within each aligned block of 32 rows no expert is named by more than 10 rows, and some block names some expert exactly 10 times.
All inputs are finite; a program needn't handle non-finite values.
Results may differ from the reference program's by a relative error of at most 0.023.
Values may be sent and summed in bfloat16 or wider, within the bound.
No kernel may reach another device: no remote copies, remote signals or barrier semaphores. Data moves between devices by JAX's collectives and lax.ppermute only.
A program may use at most 128 MiB of HBM per device.

```python
import math
import jax
import jax.numpy as jnp
import numpy as np
from jax import lax

D = 3584
FF = 1024
HD = 128
H_DEV = 2
TOP = 8
TOK_DEV = 32
HEADS = 64
EXPERTS = 32
MOST = 10
SEQ = 4096
N_CTX = 4
N_EXP = 32


def base_keys(key):
    sub_key = jax.random.fold_in(key, 11)
    table = jnp.clip(jax.random.normal(sub_key, (SEQ, HEADS * HD), jnp.float32), -4.0, 4.0)
    return table


def draw_keys(key, part):
    return base_keys(key).astype(jnp.bfloat16)


def draw_queries(key, part):
    sub_key = jax.random.fold_in(key, 23)
    table = jnp.clip(jax.random.normal(sub_key, (SEQ, HEADS * HD), jnp.float32), -4.0, 4.0)
    return table.astype(jnp.bfloat16)


def block_scale(key, dims, shards, least, largest):
    level = 1.0
    for position, parts in shards:
        steps = jax.random.uniform(jax.random.fold_in(jax.random.fold_in(key, 6), position), (parts,), jnp.float32, least / len(shards), largest / len(shards))
        level = level * jnp.repeat(jnp.exp(steps), dims[position] // parts).reshape((-1,) + (1,) * (len(dims) - 1 - position))
    return level


def deal_out(stream_key, own, number, rows, number_of, top, reach, lean):
    sequence = jax.random.permutation(stream_key, number_of)
    crowded, common = portions_of(number_of, rows * top, reach, lean, True), portions_of(number_of, rows * top, reach, lean, False)
    places = jnp.arange(number_of)

    def named(lengths, turn):
        used = int((lengths > 0).sum())
        fixed = max(1, used // 4)
        moved = fixed + (places - fixed + turn * (used - fixed)) % max(1, number_of - fixed)
        return jnp.zeros((number_of,), jnp.int32).at[sequence[jnp.where(places < fixed, places, moved)]].set(jnp.asarray(lengths, jnp.int32))

    lengths = jnp.where(number % 4 == 0, named(crowded, number // 4), named(common, number - number // 4 - 1))
    mixed = jax.random.permutation(jax.random.fold_in(own, 3), number_of)
    source_of, receiver = mixed[0:number_of // 2 * 2:2], mixed[1:number_of // 2 * 2:2]
    room = jnp.minimum(lengths[source_of] - 1, reach - lengths[receiver]) // 2
    room = jnp.where((source_of == sequence[0]) | (receiver == sequence[0]) | (lengths[receiver] == 0), 0, jnp.maximum(room, 0))
    moved = jax.random.randint(jax.random.fold_in(own, 4), (number_of // 2,), 0, 1 << 20) % (room + 1)
    lengths = lengths.at[source_of].add(-moved).at[receiver].add(moved)
    items = jnp.searchsorted(jnp.cumsum(lengths), jnp.arange(rows * top), side="right").astype(jnp.int32)
    listing = items.reshape(top, rows).T
    listing = listing[jax.random.permutation(jax.random.fold_in(own, 1), rows)]
    turn = jax.random.randint(jax.random.fold_in(own, 2), (rows, 1), 0, top)
    return jnp.take_along_axis(listing, (jnp.arange(top)[None, :] + turn) % top, axis=1)


def portions_of(amount, total, reach, slope, full):
    weights = [(1 << 20) // math.isqrt(rank ** slope) + 1 for rank in range(1, amount + 1)]
    largest = reach if full else min(reach, max(-(-total // amount), total * weights[0] // sum(weights)))
    least = 1 if total - largest >= amount - 1 else 0
    holding, surplus = [largest] + [least] * (amount - 1), total - largest - least * (amount - 1)
    while surplus > 0:
        movable = [i for i in range(1, amount) if holding[i] < largest] or [i for i in range(1, amount) if holding[i] < reach]
        whole, left = sum([weights[i] for i in movable]), surplus
        for i in movable:
            more = min(reach - holding[i], max(1, left * weights[i] // whole), surplus)
            holding[i] = holding[i] + more
            surplus = surplus - more
    return np.array(holding)


def centred(key, extent, width, bound, shards=(), held_as=jnp.bfloat16):
    entries = jax.random.normal(key, extent, jnp.float32) * width
    if len(shards) > 0:
        entries = block_scale(key, extent, shards, -0.22, 0.18) * entries
    return jnp.clip(entries, min=-bound, max=bound).astype(held_as)


def setup_inputs(seed: int = 0) -> dict:
    key_list = jax.random.split(jax.random.key(seed), 12)
    queries = draw_queries(jax.random.fold_in(key_list[11], 71), 0)
    keys = draw_keys(jax.random.fold_in(key_list[11], 71), 0)
    values = centred(key_list[2], (SEQ, HEADS * HD), 1.0, 6.0, ((0, 4), (1, 32)))
    out_proj = centred(key_list[3], (HEADS * HD, D), HD ** -0.5, 0.5, ((0, 32),))
    residual = centred(key_list[4], (SEQ, D), 1.0, 6.0, ((0, 128),))
    norm_gain = jnp.clip(1.0 + 0.15 * jax.random.normal(key_list[5], (D,), jnp.float32), 0.25, 1.75)
    routes_keys = jax.random.split(jax.random.fold_in(key_list[6], 1), SEQ // TOK_DEV)
    routes_turns = jax.random.permutation(jax.random.fold_in(key_list[6], 3), SEQ // TOK_DEV)
    routes = jax.vmap(lambda own, number: deal_out(jax.random.fold_in(key_list[6], 2), own, number, TOK_DEV, EXPERTS, TOP, MOST, 2))(routes_keys, routes_turns).reshape((SEQ, TOP))
    combine = jnp.clip(0.1 + 0.4 * jax.random.uniform(key_list[7], (SEQ, TOP), jnp.float32) ** block_scale(key_list[7], (SEQ, TOP), ((0, 128),), -0.2, 0.2), 0.1, 0.5)
    w_gate = centred(key_list[8], (EXPERTS, D, FF), D ** -0.5, 0.09375, ((0, 32), (2, 4)))
    w_up = centred(key_list[9], (EXPERTS, D, FF), D ** -0.5, 0.09375, ((0, 32), (2, 4)))
    w_down = centred(key_list[10], (EXPERTS, FF, D), FF ** -0.5, 0.1875, ((0, 32), (1, 4)))
    return dict(queries=queries, keys=keys, values=values, out_proj=out_proj, residual=residual, norm_gain=norm_gain, routes=routes, combine=combine, w_gate=w_gate, w_up=w_up, w_down=w_down)


masked_score = -1e+30
norm_eps = 1e-06

def reference(queries, keys, values, out_proj, residual, norm_gain, routes, combine, w_gate, w_up, w_down):
    scaling = 1.0 / math.sqrt(HD)
    query_heads = queries.reshape(SEQ, HEADS, HD).transpose(1, 0, 2)
    key_heads = keys.reshape(SEQ, HEADS, HD).transpose(1, 0, 2)
    value_heads = values.reshape(SEQ, HEADS, HD).transpose(1, 0, 2)
    positions = jnp.arange(SEQ)
    causal_mask = positions[:, None] >= positions[None, :]

    def one_head(triple):
        query_one, key_one, value_one = triple
        scores = jnp.dot(query_one, key_one.T, preferred_element_type=jnp.float32) * scaling
        scores = jnp.where(causal_mask, scores, masked_score)
        peak = lax.optimization_barrier(jnp.max(scores, axis=1, keepdims=True))
        expo = jnp.exp(scores - peak)
        probs = expo.astype(jnp.bfloat16)
        summed = jnp.dot(probs, value_one, preferred_element_type=jnp.float32)
        return (summed / lax.optimization_barrier(jnp.sum(expo, axis=1, keepdims=True))).astype(jnp.bfloat16)
    head_outs = lax.map(one_head, (query_heads, key_heads, value_heads))
    attended = head_outs.transpose(1, 0, 2).reshape(SEQ, HEADS * HD)
    group_width = H_DEV * HD

    def add_group(group, total):
        cols = lax.dynamic_slice_in_dim(attended, group * group_width, group_width, 1)
        rows = lax.dynamic_slice_in_dim(out_proj, group * group_width, group_width, 0)
        term = jnp.dot(cols, rows, preferred_element_type=jnp.float32)
        term = lax.optimization_barrier(term.astype(jnp.bfloat16)).astype(jnp.float32)
        return total + term
    mixed = lax.fori_loop(0, N_EXP, add_group, jnp.zeros((SEQ, D), jnp.float32))
    stream = residual.astype(jnp.float32) + mixed
    normed = (stream * lax.rsqrt(lax.optimization_barrier(jnp.mean(stream * stream, axis=1, keepdims=True)) + norm_eps) * norm_gain).astype(jnp.bfloat16)
    block_count = SEQ // TOK_DEV
    pair_count = TOK_DEV * TOP
    flat_routes = routes.reshape(block_count, pair_count).astype(jnp.int32)
    expert_hot = (flat_routes[:, :, None] == jnp.arange(EXPERTS).astype(jnp.int32)[None, None, :]).astype(jnp.int32)
    earlier = jnp.cumsum(expert_hot, axis=1).astype(jnp.int32) - expert_hot
    slot_index = lax.optimization_barrier(jnp.sum(earlier * expert_hot, axis=2)).astype(jnp.int32)
    block_index = jnp.broadcast_to(jnp.arange(block_count).astype(jnp.int32)[:, None], (block_count, pair_count))
    token_index = block_index * TOK_DEV + (jnp.arange(pair_count).astype(jnp.int32) // TOP)[None, :]
    token_rows = normed[token_index]
    buffer = jnp.zeros((EXPERTS, block_count, MOST, D), jnp.bfloat16)
    buffer = buffer.at[flat_routes, block_index, slot_index].set(token_rows)
    quarter = FF // N_CTX

    def one_expert(group):
        expert_rows, gate_weight, up_weight, down_weight = group
        row_block = expert_rows.reshape(block_count * MOST, D)
        gate = jnp.dot(row_block, gate_weight, preferred_element_type=jnp.float32)
        upper = jnp.dot(row_block, up_weight, preferred_element_type=jnp.float32)
        act = (jax.nn.silu(gate) * upper).astype(jnp.bfloat16)
        total = jnp.zeros((block_count * MOST, D), jnp.float32)
        for part_index in range(N_CTX):
            part = jnp.dot(act[:, part_index * quarter:(part_index + 1) * quarter], down_weight[part_index * quarter:(part_index + 1) * quarter], preferred_element_type=jnp.float32)
            part = lax.optimization_barrier(part.astype(jnp.bfloat16)).astype(jnp.float32)
            total = total + part
        return total.astype(jnp.bfloat16).reshape(block_count, MOST, D)
    expert_out = lax.map(one_expert, (buffer, w_gate, w_up, w_down))
    picked = expert_out[flat_routes, block_index, slot_index].astype(jnp.float32)
    weighted = picked * combine.reshape(block_count, pair_count)[:, :, None]
    moe_sum = lax.optimization_barrier(jnp.sum(weighted.reshape(block_count, TOK_DEV, TOP, D), axis=2)).reshape(SEQ, D)
    return (stream + moe_sum).astype(jnp.bfloat16)
```

```python
import math

import jax
import jax.numpy as jnp
from jax import lax
from jax.sharding import PartitionSpec as P

HD = 128


masked_score = -1e30
norm_eps = 1e-06


def from_behind(shard, axis, by):
    peers = lax.axis_size(axis)
    pairs = [(i, i + by) for i in range(peers) if 0 <= i + by < peers]
    return lax.ppermute(shard, axis, pairs)


def per_device(
    queries, keys, values, out_proj, residual, norm_gain, routes, combine, w_gate, w_up, w_down
):
    query_rows = queries.shape[0]
    head_count = queries.shape[1] // HD
    scaling = 1.0 / math.sqrt(HD)
    ctx_where = lax.axis_index("ctx")
    ctx_count = lax.axis_size("ctx")

    def attend(carried, query_heads, pair_block, visible):
        key_count = pair_block.shape[1]
        key_heads = pair_block[0].reshape(key_count, head_count, HD)
        value_heads = pair_block[1].reshape(key_count, head_count, HD)
        scores = (
            jnp.einsum("qhd,khd->hqk", query_heads, key_heads, preferred_element_type=jnp.float32)
            * scaling
        )
        scores = jnp.where(visible, scores, masked_score)
        peak_old, total_old, weighted_old = carried
        peak_new = jnp.maximum(peak_old, jnp.max(scores, axis=2))
        expo_block = jnp.exp(scores - peak_new[:, :, None])
        factor = jnp.exp(peak_old - peak_new)
        total_new = total_old * factor + jnp.sum(expo_block, axis=2)
        weighted_new = weighted_old * factor.T[:, :, None] + jnp.einsum(
            "hqk,khd->qhd",
            expo_block.astype(jnp.bfloat16),
            value_heads,
            preferred_element_type=jnp.float32,
        )
        return (peak_new, total_new, weighted_new)

    initial = (
        jnp.full((head_count, query_rows), masked_score, jnp.float32),
        jnp.zeros((head_count, query_rows), jnp.float32),
        jnp.zeros((query_rows, head_count, HD), jnp.float32),
    )
    query_heads = queries.reshape(query_rows, head_count, HD)
    row_ids = jnp.arange(query_rows)
    diag_mask = row_ids[:, None] >= row_ids[None, :]
    pair_block = jnp.stack([keys, values])
    carried = attend(initial, query_heads, pair_block, diag_mask)
    for step_index in range(1, ctx_count):
        pair_block = from_behind(pair_block, "ctx", 1)
        carried = attend(carried, query_heads, pair_block, ctx_where >= step_index)
    attended = (
        (carried[2] / carried[1].T[:, :, None])
        .astype(jnp.bfloat16)
        .reshape(query_rows, head_count * HD)
    )
    tok_count = residual.shape[0]
    term = jnp.dot(attended, out_proj, preferred_element_type=jnp.float32)
    exp_count = lax.axis_size("exp")
    group_terms = lax.all_to_all(
        term.astype(jnp.bfloat16).reshape(exp_count, query_rows // exp_count, term.shape[1]),
        "exp",
        split_axis=0,
        concat_axis=0,
        tiled=True,
    )
    mixed = jnp.sum(group_terms.astype(jnp.float32), axis=0)
    stream = residual.astype(jnp.float32) + mixed
    normed = (
        stream * lax.rsqrt(jnp.mean(stream * stream, axis=1, keepdims=True) + norm_eps) * norm_gain
    ).astype(jnp.bfloat16)
    width = normed.shape[1]
    per_token = routes.shape[1]
    experts = lax.axis_size("exp")
    capacity = min(tok_count, max(2, tok_count * per_token * 5 // (4 * experts)))
    pair_count = tok_count * per_token
    flat_routes = routes.reshape(pair_count)
    expert_hot = (flat_routes[:, None] == jnp.arange(experts)[None, :]).astype(jnp.int32)
    earlier = jnp.cumsum(expert_hot, axis=0) - expert_hot
    slot_index = jnp.sum(earlier * expert_hot, axis=1)
    position = flat_routes * capacity + slot_index
    position_hot = (position[:, None] == jnp.arange(experts * capacity)[None, :]).astype(
        jnp.float32
    )
    token_hot = (
        (jnp.arange(pair_count) // per_token)[:, None] == jnp.arange(tok_count)[None, :]
    ).astype(jnp.float32)
    pick_rows = jnp.einsum("pr,pt->rt", position_hot, token_hot).astype(jnp.bfloat16)
    outgoing = (
        jnp.dot(pick_rows, normed, preferred_element_type=jnp.float32)
        .astype(jnp.bfloat16)
        .reshape(experts, capacity, width)
    )
    received = lax.all_to_all(outgoing, "exp", split_axis=0, concat_axis=0, tiled=True)
    gate_local = w_gate[0]
    up_local = w_up[0]
    down_local = w_down[0]
    piece = lax.all_gather(received, "ctx", axis=0, tiled=True)
    gate = jnp.einsum("smd,df->smf", piece, gate_local, preferred_element_type=jnp.float32)
    upper = jnp.einsum("smd,df->smf", piece, up_local, preferred_element_type=jnp.float32)
    act_all = (jax.nn.silu(gate) * upper).astype(jnp.bfloat16)
    expert_out = lax.psum_scatter(
        jnp.einsum("smf,fd->smd", act_all, down_local, preferred_element_type=jnp.float32).astype(
            jnp.bfloat16
        ),
        "ctx",
        scatter_dimension=0,
        tiled=True,
    )
    returned = lax.all_to_all(expert_out, "exp", split_axis=0, concat_axis=0, tiled=True)
    weigh_rows = jnp.einsum(
        "pr,pt->tr", position_hot, token_hot * combine.reshape(pair_count)[:, None]
    )
    moe_sum = jnp.dot(
        weigh_rows,
        returned.reshape(experts * capacity, width).astype(jnp.float32),
        precision=lax.Precision.HIGHEST,
    )
    return (stream + moe_sum).astype(jnp.bfloat16)


def solution(mesh):
    in_specs = (
        P("ctx", "exp"),
        P("ctx", "exp"),
        P("ctx", "exp"),
        P("exp", None),
        P(("ctx", "exp"), None),
        P(),
        P(("ctx", "exp"), None),
        P(("ctx", "exp"), None),
        P("exp", None, "ctx"),
        P("exp", None, "ctx"),
        P("exp", "ctx", None),
    )
    out_specs = P(("ctx", "exp"), None)
    return jax.shard_map(
        per_device, mesh=mesh, in_specs=in_specs, out_specs=out_specs, check_vma=False
    )
```

```python
import math

import jax
import jax.numpy as jnp
from jax import lax
from jax.sharding import PartitionSpec as P

HD = 128


masked_score = -1e30
norm_eps = 1e-06


def from_behind(shard, axis, by):
    peers = lax.axis_size(axis)
    pairs = [(i, i + by) for i in range(peers) if 0 <= i + by < peers]
    return lax.ppermute(shard, axis, pairs)


def per_device(
    queries, keys, values, out_proj, residual, norm_gain, routes, combine, w_gate, w_up, w_down
):
    query_rows = queries.shape[0]
    head_count = queries.shape[1] // HD
    scaling = 1.0 / math.sqrt(HD)
    ctx_where = lax.axis_index("ctx")
    ctx_count = lax.axis_size("ctx")

    def attend(carried, query_heads, pair_block, visible):
        key_count = pair_block.shape[1]
        key_heads = pair_block[0].reshape(key_count, head_count, HD)
        value_heads = pair_block[1].reshape(key_count, head_count, HD)
        scores = (
            jnp.einsum("qhd,khd->hqk", query_heads, key_heads, preferred_element_type=jnp.float32)
            * scaling
        )
        scores = jnp.where(visible, scores, masked_score)
        peak_old, total_old, weighted_old = carried
        peak_new = jnp.maximum(peak_old, jnp.max(scores, axis=2))
        expo_block = jnp.exp(scores - peak_new[:, :, None])
        factor = jnp.exp(peak_old - peak_new)
        total_new = total_old * factor + jnp.sum(expo_block, axis=2)
        weighted_new = weighted_old * factor.T[:, :, None] + jnp.einsum(
            "hqk,khd->qhd",
            expo_block.astype(jnp.bfloat16),
            value_heads,
            preferred_element_type=jnp.float32,
        )
        return (peak_new, total_new, weighted_new)

    initial = (
        jnp.full((head_count, query_rows), masked_score, jnp.float32),
        jnp.zeros((head_count, query_rows), jnp.float32),
        jnp.zeros((query_rows, head_count, HD), jnp.float32),
    )
    query_heads = queries.reshape(query_rows, head_count, HD)
    row_ids = jnp.arange(query_rows)
    diag_mask = row_ids[:, None] >= row_ids[None, :]
    pair_block = jnp.stack([keys, values])
    carried = attend(initial, query_heads, pair_block, diag_mask)
    for step_index in range(1, ctx_count):
        pair_block = from_behind(pair_block, "ctx", 1)
        carried = attend(carried, query_heads, pair_block, ctx_where >= step_index)
    attended = (
        (carried[2] / carried[1].T[:, :, None])
        .astype(jnp.bfloat16)
        .reshape(query_rows, head_count * HD)
    )
    tok_count = residual.shape[0]
    term = jnp.dot(attended, out_proj, preferred_element_type=jnp.float32)
    exp_count = lax.axis_size("exp")
    group_terms = lax.all_to_all(
        term.astype(jnp.bfloat16).reshape(exp_count, query_rows // exp_count, term.shape[1]),
        "exp",
        split_axis=0,
        concat_axis=0,
        tiled=True,
    )
    mixed = jnp.sum(group_terms.astype(jnp.float32), axis=0)
    stream = residual.astype(jnp.float32) + mixed
    normed = (
        stream * lax.rsqrt(jnp.mean(stream * stream, axis=1, keepdims=True) + norm_eps) * norm_gain
    ).astype(jnp.bfloat16)
    width = normed.shape[1]
    per_token = routes.shape[1]
    experts = lax.axis_size("exp")
    capacity = min(tok_count, max(2, tok_count * per_token * 5 // (4 * experts)))
    pair_count = tok_count * per_token
    flat_routes = routes.reshape(pair_count)
    expert_hot = (flat_routes[:, None] == jnp.arange(experts)[None, :]).astype(jnp.int32)
    earlier = jnp.cumsum(expert_hot, axis=0) - expert_hot
    slot_index = jnp.sum(earlier * expert_hot, axis=1)
    position = flat_routes * capacity + slot_index
    position_hot = (position[:, None] == jnp.arange(experts * capacity)[None, :]).astype(
        jnp.float32
    )
    token_hot = (
        (jnp.arange(pair_count) // per_token)[:, None] == jnp.arange(tok_count)[None, :]
    ).astype(jnp.float32)
    pick_rows = jnp.einsum("pr,pt->rt", position_hot, token_hot).astype(jnp.bfloat16)
    outgoing = (
        jnp.dot(pick_rows, normed, preferred_element_type=jnp.float32)
        .astype(jnp.bfloat16)
        .reshape(experts, capacity, width)
    )
    received = lax.all_to_all(outgoing, "exp", split_axis=0, concat_axis=0, tiled=True)
    gate_full = lax.all_gather(w_gate[0], "ctx", axis=1, tiled=True)
    up_full = lax.all_gather(w_up[0], "ctx", axis=1, tiled=True)
    down_full = lax.all_gather(w_down[0], "ctx", axis=0, tiled=True)
    rows = received.reshape(experts * capacity, width)
    gate = jnp.dot(rows, gate_full, preferred_element_type=jnp.float32)
    upper = jnp.dot(rows, up_full, preferred_element_type=jnp.float32)
    act_all = (jax.nn.silu(gate) * upper).astype(jnp.bfloat16)
    quarter = w_down.shape[1]
    quarter_terms = jnp.einsum(
        "rqf,qfd->qrd",
        act_all.reshape(experts * capacity, ctx_count, quarter),
        down_full.reshape(ctx_count, quarter, width),
        preferred_element_type=jnp.float32,
    ).astype(jnp.bfloat16)
    expert_out = (
        jnp.sum(quarter_terms.astype(jnp.float32), axis=0)
        .astype(jnp.bfloat16)
        .reshape(experts, capacity, width)
    )
    returned = lax.all_to_all(expert_out, "exp", split_axis=0, concat_axis=0, tiled=True)
    weigh_rows = jnp.einsum(
        "pr,pt->tr", position_hot, token_hot * combine.reshape(pair_count)[:, None]
    )
    moe_sum = jnp.dot(
        weigh_rows,
        returned.reshape(experts * capacity, width).astype(jnp.float32),
        precision=lax.Precision.HIGHEST,
    )
    return (stream + moe_sum).astype(jnp.bfloat16)


def solution(mesh):
    in_specs = (
        P("ctx", "exp"),
        P("ctx", "exp"),
        P("ctx", "exp"),
        P("exp", None),
        P(("ctx", "exp"), None),
        P(),
        P(("ctx", "exp"), None),
        P(("ctx", "exp"), None),
        P("exp", None, "ctx"),
        P("exp", None, "ctx"),
        P("exp", "ctx", None),
    )
    out_specs = P(("ctx", "exp"), None)
    return jax.shard_map(
        per_device, mesh=mesh, in_specs=in_specs, out_specs=out_specs, check_vma=False
    )
```

```python
import math

import jax
import jax.numpy as jnp
from jax import lax
from jax.sharding import Mesh, PartitionSpec as P

HD = 128


CTX = ("ctx_hi", "ctx_lo")

masked_score = -1e30
norm_eps = 1e-06


def from_behind(shard, axis, by):
    peers = lax.axis_size(axis)
    pairs = [(i, i + by) for i in range(peers) if 0 <= i + by < peers]
    return lax.ppermute(shard, axis, pairs)


def per_device(
    queries, keys, values, out_proj, residual, norm_gain, routes, combine, w_gate, w_up, w_down
):
    query_rows = queries.shape[0]
    head_count = queries.shape[1] // HD
    scaling = 1.0 / math.sqrt(HD)
    ctx_where = lax.axis_index(CTX)
    ctx_count = lax.axis_size(CTX)

    def attend(carried, query_heads, pair_block, visible):
        key_count = pair_block.shape[1]
        key_heads = pair_block[0].reshape(key_count, head_count, HD)
        value_heads = pair_block[1].reshape(key_count, head_count, HD)
        scores = (
            jnp.einsum("qhd,khd->hqk", query_heads, key_heads, preferred_element_type=jnp.float32)
            * scaling
        )
        scores = jnp.where(visible, scores, masked_score)
        peak_old, total_old, weighted_old = carried
        peak_new = jnp.maximum(peak_old, jnp.max(scores, axis=2))
        expo_block = jnp.exp(scores - peak_new[:, :, None])
        factor = jnp.exp(peak_old - peak_new)
        total_new = total_old * factor + jnp.sum(expo_block, axis=2)
        weighted_new = weighted_old * factor.T[:, :, None] + jnp.einsum(
            "hqk,khd->qhd",
            expo_block.astype(jnp.bfloat16),
            value_heads,
            preferred_element_type=jnp.float32,
        )
        return (peak_new, total_new, weighted_new)

    initial = (
        jnp.full((head_count, query_rows), masked_score, jnp.float32),
        jnp.zeros((head_count, query_rows), jnp.float32),
        jnp.zeros((query_rows, head_count, HD), jnp.float32),
    )
    query_heads = queries.reshape(query_rows, head_count, HD)
    row_ids = jnp.arange(query_rows)
    diag_mask = row_ids[:, None] >= row_ids[None, :]
    pair_block = jnp.stack([keys, values])
    carried = attend(initial, query_heads, pair_block, diag_mask)
    for step_index in range(1, ctx_count):
        pair_block = from_behind(pair_block, CTX, 1)
        carried = attend(carried, query_heads, pair_block, ctx_where >= step_index)
    attended = (
        (carried[2] / carried[1].T[:, :, None])
        .astype(jnp.bfloat16)
        .reshape(query_rows, head_count * HD)
    )
    tok_count = residual.shape[0]
    term = jnp.dot(attended, out_proj, preferred_element_type=jnp.float32)
    exp_count = lax.axis_size("exp")
    group_terms = lax.all_to_all(
        term.astype(jnp.bfloat16).reshape(exp_count, query_rows // exp_count, term.shape[1]),
        "exp",
        split_axis=0,
        concat_axis=0,
        tiled=True,
    )
    mixed = jnp.sum(group_terms.astype(jnp.float32), axis=0)
    stream = residual.astype(jnp.float32) + mixed
    normed = (
        stream * lax.rsqrt(jnp.mean(stream * stream, axis=1, keepdims=True) + norm_eps) * norm_gain
    ).astype(jnp.bfloat16)
    width = normed.shape[1]
    per_token = routes.shape[1]
    experts = lax.axis_size("exp")
    capacity = min(tok_count, max(2, tok_count * per_token * 5 // (4 * experts)))
    pair_count = tok_count * per_token
    flat_routes = routes.reshape(pair_count)
    expert_hot = (flat_routes[:, None] == jnp.arange(experts)[None, :]).astype(jnp.int32)
    earlier = jnp.cumsum(expert_hot, axis=0) - expert_hot
    slot_index = jnp.sum(earlier * expert_hot, axis=1)
    position = flat_routes * capacity + slot_index
    position_hot = (position[:, None] == jnp.arange(experts * capacity)[None, :]).astype(
        jnp.float32
    )
    token_hot = (
        (jnp.arange(pair_count) // per_token)[:, None] == jnp.arange(tok_count)[None, :]
    ).astype(jnp.float32)
    pick_rows = jnp.einsum("pr,pt->rt", position_hot, token_hot).astype(jnp.bfloat16)
    outgoing = (
        jnp.dot(pick_rows, normed, preferred_element_type=jnp.float32)
        .astype(jnp.bfloat16)
        .reshape(experts, capacity, width)
    )
    received = lax.all_to_all(outgoing, "exp", split_axis=0, concat_axis=0, tiled=True)
    def gather_quarters(local, axis):
        across = lax.all_gather(local, "ctx_hi", axis=axis, tiled=True)
        return lax.all_gather(across, "ctx_lo", axis=axis, tiled=True)

    gate_full = gather_quarters(w_gate[0], 1)
    up_full = gather_quarters(w_up[0], 1)
    down_full = gather_quarters(w_down[0], 0)
    rows = received.reshape(experts * capacity, width)
    gate = jnp.dot(rows, gate_full, preferred_element_type=jnp.float32)
    upper = jnp.dot(rows, up_full, preferred_element_type=jnp.float32)
    act_all = (jax.nn.silu(gate) * upper).astype(jnp.bfloat16)
    quarter = w_down.shape[1]
    quarter_terms = jnp.einsum(
        "rqf,qfd->qrd",
        act_all.reshape(experts * capacity, ctx_count, quarter),
        down_full.reshape(ctx_count, quarter, width),
        preferred_element_type=jnp.float32,
    ).astype(jnp.bfloat16)
    expert_out = (
        jnp.sum(quarter_terms.astype(jnp.float32), axis=0)
        .astype(jnp.bfloat16)
        .reshape(experts, capacity, width)
    )
    returned = lax.all_to_all(expert_out, "exp", split_axis=0, concat_axis=0, tiled=True)
    weigh_rows = jnp.einsum(
        "pr,pt->tr", position_hot, token_hot * combine.reshape(pair_count)[:, None]
    )
    moe_sum = jnp.dot(
        weigh_rows,
        returned.reshape(experts * capacity, width).astype(jnp.float32),
        precision=lax.Precision.HIGHEST,
    )
    return (stream + moe_sum).astype(jnp.bfloat16)


def solution(mesh):
    in_specs = (
        P(CTX, "exp"),
        P(CTX, "exp"),
        P(CTX, "exp"),
        P("exp", None),
        P((*CTX, "exp"), None),
        P(),
        P((*CTX, "exp"), None),
        P((*CTX, "exp"), None),
        P("exp", None, CTX),
        P("exp", None, CTX),
        P("exp", CTX, None),
    )
    out_specs = P((*CTX, "exp"), None)
    split_mesh = Mesh(mesh.devices.reshape(2, 2, -1), (*CTX, "exp"))
    return jax.shard_map(
        per_device, mesh=split_mesh, in_specs=in_specs, out_specs=out_specs, check_vma=False
    )
```

```python
import math

import jax
import jax.numpy as jnp
from jax import lax
from jax.sharding import Mesh, PartitionSpec as P

HD = 128


CTX = ("ctx_hi", "ctx_lo")

masked_score = -1e30
norm_eps = 1e-06


def from_behind(shard, axis, by):
    peers = lax.axis_size(axis)
    pairs = [(i, i + by) for i in range(peers) if 0 <= i + by < peers]
    return lax.ppermute(shard, axis, pairs)


def per_device(
    queries, keys, values, out_proj, residual, norm_gain, routes, combine, w_gate, w_up, w_down
):
    query_rows = queries.shape[0]
    head_count = queries.shape[1] // HD
    scaling = 1.0 / math.sqrt(HD)
    ctx_where = lax.axis_index(CTX)
    ctx_count = lax.axis_size(CTX)

    def attend(carried, query_heads, pair_block, visible):
        key_count = pair_block.shape[1]
        key_heads = pair_block[0].reshape(key_count, head_count, HD)
        value_heads = pair_block[1].reshape(key_count, head_count, HD)
        scores = (
            jnp.einsum("qhd,khd->hqk", query_heads, key_heads, preferred_element_type=jnp.float32)
            * scaling
        )
        scores = jnp.where(visible, scores, masked_score)
        peak_old, total_old, weighted_old = carried
        peak_new = jnp.maximum(peak_old, jnp.max(scores, axis=2))
        expo_block = jnp.exp(scores - peak_new[:, :, None])
        factor = jnp.exp(peak_old - peak_new)
        total_new = total_old * factor + jnp.sum(expo_block, axis=2)
        weighted_new = weighted_old * factor.T[:, :, None] + jnp.einsum(
            "hqk,khd->qhd",
            expo_block.astype(jnp.bfloat16),
            value_heads,
            preferred_element_type=jnp.float32,
        )
        return (peak_new, total_new, weighted_new)

    initial = (
        jnp.full((head_count, query_rows), masked_score, jnp.float32),
        jnp.zeros((head_count, query_rows), jnp.float32),
        jnp.zeros((query_rows, head_count, HD), jnp.float32),
    )
    query_heads = queries.reshape(query_rows, head_count, HD)
    row_ids = jnp.arange(query_rows)
    diag_mask = row_ids[:, None] >= row_ids[None, :]
    pair_block = jnp.stack([keys, values])
    carried = attend(initial, query_heads, pair_block, diag_mask)
    for step_index in range(1, ctx_count):
        pair_block = from_behind(pair_block, CTX, 1)
        carried = attend(carried, query_heads, pair_block, ctx_where >= step_index)
    attended = (
        (carried[2] / carried[1].T[:, :, None])
        .astype(jnp.bfloat16)
        .reshape(query_rows, head_count * HD)
    )
    tok_count = residual.shape[0]
    term = jnp.dot(attended, out_proj, preferred_element_type=jnp.float32)
    exp_count = lax.axis_size("exp")
    group_terms = lax.all_to_all(
        term.astype(jnp.bfloat16).reshape(exp_count, query_rows // exp_count, term.shape[1]),
        "exp",
        split_axis=0,
        concat_axis=0,
        tiled=True,
    )
    mixed = jnp.sum(group_terms.astype(jnp.float32), axis=0)
    stream = residual.astype(jnp.float32) + mixed
    normed = (
        stream * lax.rsqrt(jnp.mean(stream * stream, axis=1, keepdims=True) + norm_eps) * norm_gain
    ).astype(jnp.bfloat16)
    width = normed.shape[1]
    per_token = routes.shape[1]
    experts = lax.axis_size("exp")
    capacity = min(tok_count, max(2, tok_count * per_token * 5 // (4 * experts)))
    pair_count = tok_count * per_token
    flat_routes = routes.reshape(pair_count)
    expert_hot = (flat_routes[:, None] == jnp.arange(experts)[None, :]).astype(jnp.int32)
    earlier = jnp.cumsum(expert_hot, axis=0) - expert_hot
    slot_index = jnp.sum(earlier * expert_hot, axis=1)
    position = flat_routes * capacity + slot_index
    position_hot = (position[:, None] == jnp.arange(experts * capacity)[None, :]).astype(
        jnp.float32
    )
    token_hot = (
        (jnp.arange(pair_count) // per_token)[:, None] == jnp.arange(tok_count)[None, :]
    ).astype(jnp.float32)
    pick_rows = jnp.einsum("pr,pt->rt", position_hot, token_hot).astype(jnp.bfloat16)
    outgoing = (
        jnp.dot(pick_rows, normed, preferred_element_type=jnp.float32)
        .astype(jnp.bfloat16)
        .reshape(experts, capacity, width)
    )
    received = lax.all_to_all(outgoing, "exp", split_axis=0, concat_axis=0, tiled=True)
    def gather_quarters(local, axis):
        swap = [(0, 1), (1, 0)]
        across = jnp.concatenate([local, lax.ppermute(local, "ctx_hi", swap)], axis=axis)
        return jnp.concatenate([across, lax.ppermute(across, "ctx_lo", swap)], axis=axis)

    gate_full = gather_quarters(w_gate[0], 1)
    up_full = gather_quarters(w_up[0], 1)
    down_full = gather_quarters(w_down[0], 0)
    rows = received.reshape(experts * capacity, width)
    gate = jnp.dot(rows, gate_full, preferred_element_type=jnp.float32)
    upper = jnp.dot(rows, up_full, preferred_element_type=jnp.float32)
    act_all = (jax.nn.silu(gate) * upper).astype(jnp.bfloat16)
    quarter = w_down.shape[1]
    quarter_terms = jnp.einsum(
        "rqf,qfd->qrd",
        act_all.reshape(experts * capacity, ctx_count, quarter),
        down_full.reshape(ctx_count, quarter, width),
        preferred_element_type=jnp.float32,
    ).astype(jnp.bfloat16)
    expert_out = (
        jnp.sum(quarter_terms.astype(jnp.float32), axis=0)
        .astype(jnp.bfloat16)
        .reshape(experts, capacity, width)
    )
    returned = lax.all_to_all(expert_out, "exp", split_axis=0, concat_axis=0, tiled=True)
    weigh_rows = jnp.einsum(
        "pr,pt->tr", position_hot, token_hot * combine.reshape(pair_count)[:, None]
    )
    moe_sum = jnp.dot(
        weigh_rows,
        returned.reshape(experts * capacity, width).astype(jnp.float32),
        precision=lax.Precision.HIGHEST,
    )
    return (stream + moe_sum).astype(jnp.bfloat16)


def solution(mesh):
    in_specs = (
        P(CTX, "exp"),
        P(CTX, "exp"),
        P(CTX, "exp"),
        P("exp", None),
        P((*CTX, "exp"), None),
        P(),
        P((*CTX, "exp"), None),
        P((*CTX, "exp"), None),
        P("exp", None, CTX),
        P("exp", None, CTX),
        P("exp", CTX, None),
    )
    out_specs = P((*CTX, "exp"), None)
    split_mesh = Mesh(mesh.devices.reshape(2, 2, -1), (*CTX, "exp"))
    return jax.shard_map(
        per_device, mesh=split_mesh, in_specs=in_specs, out_specs=out_specs, check_vma=False
    )
```

```python
import math

import jax
import jax.numpy as jnp
from jax import lax
from jax.sharding import PartitionSpec as P

HD = 128


masked_score = -1e30
norm_eps = 1e-06


def from_behind(shard, axis, by):
    peers = lax.axis_size(axis)
    pairs = [(i, i + by) for i in range(peers) if 0 <= i + by < peers]
    return lax.ppermute(shard, axis, pairs)


def per_device(
    queries, keys, values, out_proj, residual, norm_gain, routes, combine, w_gate, w_up, w_down
):
    query_rows = queries.shape[0]
    head_count = queries.shape[1] // HD
    scaling = 1.0 / math.sqrt(HD)
    ctx_where = lax.axis_index("ctx")
    ctx_count = lax.axis_size("ctx")

    def attend(carried, query_heads, pair_block, visible):
        key_count = pair_block.shape[1]
        key_heads = pair_block[0].reshape(key_count, head_count, HD)
        value_heads = pair_block[1].reshape(key_count, head_count, HD)
        scores = (
            jnp.einsum("qhd,khd->hqk", query_heads, key_heads, preferred_element_type=jnp.float32)
            * scaling
        )
        scores = jnp.where(visible, scores, masked_score)
        peak_old, total_old, weighted_old = carried
        peak_new = jnp.maximum(peak_old, jnp.max(scores, axis=2))
        expo_block = jnp.exp(scores - peak_new[:, :, None])
        factor = jnp.exp(peak_old - peak_new)
        total_new = total_old * factor + jnp.sum(expo_block, axis=2)
        weighted_new = weighted_old * factor.T[:, :, None] + jnp.einsum(
            "hqk,khd->qhd",
            expo_block.astype(jnp.bfloat16),
            value_heads,
            preferred_element_type=jnp.float32,
        )
        return (peak_new, total_new, weighted_new)

    initial = (
        jnp.full((head_count, query_rows), masked_score, jnp.float32),
        jnp.zeros((head_count, query_rows), jnp.float32),
        jnp.zeros((query_rows, head_count, HD), jnp.float32),
    )
    query_heads = queries.reshape(query_rows, head_count, HD)
    row_ids = jnp.arange(query_rows)
    diag_mask = row_ids[:, None] >= row_ids[None, :]
    pair_block = jnp.stack([keys, values])
    carried = attend(initial, query_heads, pair_block, diag_mask)
    for step_index in range(1, ctx_count):
        pair_block = from_behind(pair_block, "ctx", 1)
        carried = attend(carried, query_heads, pair_block, ctx_where >= step_index)
    attended = (
        (carried[2] / carried[1].T[:, :, None])
        .astype(jnp.bfloat16)
        .reshape(query_rows, head_count * HD)
    )
    tok_count = residual.shape[0]
    term = jnp.dot(attended, out_proj, preferred_element_type=jnp.float32)
    exp_count = lax.axis_size("exp")
    group_terms = lax.all_to_all(
        term.astype(jnp.bfloat16).reshape(exp_count, query_rows // exp_count, term.shape[1]),
        "exp",
        split_axis=0,
        concat_axis=0,
        tiled=True,
    )
    mixed = jnp.sum(group_terms.astype(jnp.float32), axis=0)
    stream = residual.astype(jnp.float32) + mixed
    normed = (
        stream * lax.rsqrt(jnp.mean(stream * stream, axis=1, keepdims=True) + norm_eps) * norm_gain
    ).astype(jnp.bfloat16)
    width = normed.shape[1]
    per_token = routes.shape[1]
    experts = lax.axis_size("exp")
    capacity = min(tok_count, max(2, tok_count * per_token * 5 // (4 * experts)))
    pair_count = tok_count * per_token
    flat_routes = routes.reshape(pair_count)
    expert_hot = (flat_routes[:, None] == jnp.arange(experts)[None, :]).astype(jnp.int32)
    earlier = jnp.cumsum(expert_hot, axis=0) - expert_hot
    slot_index = jnp.sum(earlier * expert_hot, axis=1)
    position = flat_routes * capacity + slot_index
    position_hot = (position[:, None] == jnp.arange(experts * capacity)[None, :]).astype(
        jnp.float32
    )
    token_hot = (
        (jnp.arange(pair_count) // per_token)[:, None] == jnp.arange(tok_count)[None, :]
    ).astype(jnp.float32)
    pick_rows = jnp.einsum("pr,pt->rt", position_hot, token_hot).astype(jnp.bfloat16)
    outgoing = (
        jnp.dot(pick_rows, normed, preferred_element_type=jnp.float32)
        .astype(jnp.bfloat16)
        .reshape(experts, 8, capacity * width // 8)
    )
    received = lax.all_to_all(outgoing, "exp", split_axis=0, concat_axis=0, tiled=True)
    gate_full = lax.all_gather(w_gate[0], "ctx", axis=1, tiled=True)
    up_full = lax.all_gather(w_up[0], "ctx", axis=1, tiled=True)
    down_full = lax.all_gather(w_down[0], "ctx", axis=0, tiled=True)
    rows = received.reshape(experts * capacity, width)
    gate = jnp.dot(rows, gate_full, preferred_element_type=jnp.float32)
    upper = jnp.dot(rows, up_full, preferred_element_type=jnp.float32)
    act_all = (jax.nn.silu(gate) * upper).astype(jnp.bfloat16)
    quarter = w_down.shape[1]
    quarter_terms = jnp.einsum(
        "rqf,qfd->qrd",
        act_all.reshape(experts * capacity, ctx_count, quarter),
        down_full.reshape(ctx_count, quarter, width),
        preferred_element_type=jnp.float32,
    ).astype(jnp.bfloat16)
    expert_out = (
        jnp.sum(quarter_terms.astype(jnp.float32), axis=0)
        .astype(jnp.bfloat16)
        .reshape(experts, 8, capacity * width // 8)
    )
    returned = lax.all_to_all(expert_out, "exp", split_axis=0, concat_axis=0, tiled=True)
    weigh_rows = jnp.einsum(
        "pr,pt->tr", position_hot, token_hot * combine.reshape(pair_count)[:, None]
    )
    moe_sum = jnp.dot(
        weigh_rows,
        returned.reshape(experts * capacity, width).astype(jnp.float32),
        precision=lax.Precision.HIGHEST,
    )
    return (stream + moe_sum).astype(jnp.bfloat16)


def solution(mesh):
    in_specs = (
        P("ctx", "exp"),
        P("ctx", "exp"),
        P("ctx", "exp"),
        P("exp", None),
        P(("ctx", "exp"), None),
        P(),
        P(("ctx", "exp"), None),
        P(("ctx", "exp"), None),
        P("exp", None, "ctx"),
        P("exp", None, "ctx"),
        P("exp", "ctx", None),
    )
    out_specs = P(("ctx", "exp"), None)
    return jax.shard_map(
        per_device, mesh=mesh, in_specs=in_specs, out_specs=out_specs, check_vma=False
    )
```

```python
import math

import jax
import jax.numpy as jnp
from jax import lax
from jax.sharding import PartitionSpec as P

HD = 128


masked_score = -1e30
norm_eps = 1e-06


def from_behind(shard, axis, by):
    peers = lax.axis_size(axis)
    pairs = [(i, i + by) for i in range(peers) if 0 <= i + by < peers]
    return lax.ppermute(shard, axis, pairs)


def per_device(
    queries, keys, values, out_proj, residual, norm_gain, routes, combine, w_gate, w_up, w_down
):
    query_rows = queries.shape[0]
    head_count = queries.shape[1] // HD
    scaling = 1.0 / math.sqrt(HD)
    ctx_where = lax.axis_index("ctx")
    ctx_count = lax.axis_size("ctx")

    def attend(carried, query_heads, pair_block, visible):
        key_count = pair_block.shape[1]
        key_heads = pair_block[0].reshape(key_count, head_count, HD)
        value_heads = pair_block[1].reshape(key_count, head_count, HD)
        scores = (
            jnp.einsum("qhd,khd->hqk", query_heads, key_heads, preferred_element_type=jnp.float32)
            * scaling
        )
        scores = jnp.where(visible, scores, masked_score)
        peak_old, total_old, weighted_old = carried
        peak_new = jnp.maximum(peak_old, jnp.max(scores, axis=2))
        expo_block = jnp.exp(scores - peak_new[:, :, None])
        factor = jnp.exp(peak_old - peak_new)
        total_new = total_old * factor + jnp.sum(expo_block, axis=2)
        weighted_new = weighted_old * factor.T[:, :, None] + jnp.einsum(
            "hqk,khd->qhd",
            expo_block.astype(jnp.bfloat16),
            value_heads,
            preferred_element_type=jnp.float32,
        )
        return (peak_new, total_new, weighted_new)

    initial = (
        jnp.full((head_count, query_rows), masked_score, jnp.float32),
        jnp.zeros((head_count, query_rows), jnp.float32),
        jnp.zeros((query_rows, head_count, HD), jnp.float32),
    )
    query_heads = queries.reshape(query_rows, head_count, HD)
    row_ids = jnp.arange(query_rows)
    diag_mask = row_ids[:, None] >= row_ids[None, :]
    pair_block = jnp.stack([keys, values])
    earlier_blocks = [from_behind(pair_block, "ctx", step) for step in range(1, ctx_count)]
    carried = attend(initial, query_heads, pair_block, diag_mask)
    for step_index in range(1, ctx_count):
        carried = attend(
            carried, query_heads, earlier_blocks[step_index - 1], ctx_where >= step_index
        )
    attended = (
        (carried[2] / carried[1].T[:, :, None])
        .astype(jnp.bfloat16)
        .reshape(query_rows, head_count * HD)
    )
    tok_count = residual.shape[0]
    term = jnp.dot(attended, out_proj, preferred_element_type=jnp.float32)
    exp_count = lax.axis_size("exp")
    group_terms = lax.all_to_all(
        term.astype(jnp.bfloat16).reshape(exp_count, query_rows // exp_count, term.shape[1]),
        "exp",
        split_axis=0,
        concat_axis=0,
        tiled=True,
    )
    mixed = jnp.sum(group_terms.astype(jnp.float32), axis=0)
    stream = residual.astype(jnp.float32) + mixed
    normed = (
        stream * lax.rsqrt(jnp.mean(stream * stream, axis=1, keepdims=True) + norm_eps) * norm_gain
    ).astype(jnp.bfloat16)
    width = normed.shape[1]
    per_token = routes.shape[1]
    experts = lax.axis_size("exp")
    capacity = min(tok_count, max(2, tok_count * per_token * 5 // (4 * experts)))
    pair_count = tok_count * per_token
    flat_routes = routes.reshape(pair_count)
    expert_hot = (flat_routes[:, None] == jnp.arange(experts)[None, :]).astype(jnp.int32)
    earlier = jnp.cumsum(expert_hot, axis=0) - expert_hot
    slot_index = jnp.sum(earlier * expert_hot, axis=1)
    position = flat_routes * capacity + slot_index
    position_hot = (position[:, None] == jnp.arange(experts * capacity)[None, :]).astype(
        jnp.float32
    )
    token_hot = (
        (jnp.arange(pair_count) // per_token)[:, None] == jnp.arange(tok_count)[None, :]
    ).astype(jnp.float32)
    pick_rows = jnp.einsum("pr,pt->rt", position_hot, token_hot).astype(jnp.bfloat16)
    outgoing = (
        jnp.dot(pick_rows, normed, preferred_element_type=jnp.float32)
        .astype(jnp.bfloat16)
        .reshape(experts, 8, capacity * width // 8)
    )
    received = lax.all_to_all(outgoing, "exp", split_axis=0, concat_axis=0, tiled=True)
    gate_full = lax.all_gather(w_gate[0], "ctx", axis=1, tiled=True)
    up_full = lax.all_gather(w_up[0], "ctx", axis=1, tiled=True)
    down_full = lax.all_gather(w_down[0], "ctx", axis=0, tiled=True)
    rows = received.reshape(experts * capacity, width)
    gate = jnp.dot(rows, gate_full, preferred_element_type=jnp.float32)
    upper = jnp.dot(rows, up_full, preferred_element_type=jnp.float32)
    act_all = (jax.nn.silu(gate) * upper).astype(jnp.bfloat16)
    quarter = w_down.shape[1]
    quarter_terms = jnp.einsum(
        "rqf,qfd->qrd",
        act_all.reshape(experts * capacity, ctx_count, quarter),
        down_full.reshape(ctx_count, quarter, width),
        preferred_element_type=jnp.float32,
    ).astype(jnp.bfloat16)
    expert_out = (
        jnp.sum(quarter_terms.astype(jnp.float32), axis=0)
        .astype(jnp.bfloat16)
        .reshape(experts, 8, capacity * width // 8)
    )
    returned = lax.all_to_all(expert_out, "exp", split_axis=0, concat_axis=0, tiled=True)
    weigh_rows = jnp.einsum(
        "pr,pt->tr", position_hot, token_hot * combine.reshape(pair_count)[:, None]
    )
    moe_sum = jnp.dot(
        weigh_rows,
        returned.reshape(experts * capacity, width).astype(jnp.float32),
        precision=lax.Precision.HIGHEST,
    )
    return (stream + moe_sum).astype(jnp.bfloat16)


def solution(mesh):
    in_specs = (
        P("ctx", "exp"),
        P("ctx", "exp"),
        P("ctx", "exp"),
        P("exp", None),
        P(("ctx", "exp"), None),
        P(),
        P(("ctx", "exp"), None),
        P(("ctx", "exp"), None),
        P("exp", None, "ctx"),
        P("exp", None, "ctx"),
        P("exp", "ctx", None),
    )
    out_specs = P(("ctx", "exp"), None)
    return jax.shard_map(
        per_device, mesh=mesh, in_specs=in_specs, out_specs=out_specs, check_vma=False
    )
```

```python
import math

import jax
import jax.numpy as jnp
from jax import lax
from jax.sharding import Mesh, PartitionSpec as P

HD = 128


CTX = ("ctx_hi", "ctx_lo")

masked_score = -1e30
norm_eps = 1e-06


def from_behind(shard, axis, by):
    peers = lax.axis_size(axis)
    pairs = [(i, i + by) for i in range(peers) if 0 <= i + by < peers]
    return lax.ppermute(shard, axis, pairs)


def per_device(
    queries, keys, values, out_proj, residual, norm_gain, routes, combine, w_gate, w_up, w_down
):
    query_rows = queries.shape[0]
    head_count = queries.shape[1] // HD
    scaling = 1.0 / math.sqrt(HD)
    ctx_where = lax.axis_index(CTX)
    ctx_count = lax.axis_size(CTX)

    def attend(carried, query_heads, pair_block, visible):
        key_count = pair_block.shape[1]
        key_heads = pair_block[0].reshape(key_count, head_count, HD)
        value_heads = pair_block[1].reshape(key_count, head_count, HD)
        scores = (
            jnp.einsum("qhd,khd->hqk", query_heads, key_heads, preferred_element_type=jnp.float32)
            * scaling
        )
        scores = jnp.where(visible, scores, masked_score)
        peak_old, total_old, weighted_old = carried
        peak_new = jnp.maximum(peak_old, jnp.max(scores, axis=2))
        expo_block = jnp.exp(scores - peak_new[:, :, None])
        factor = jnp.exp(peak_old - peak_new)
        total_new = total_old * factor + jnp.sum(expo_block, axis=2)
        weighted_new = weighted_old * factor.T[:, :, None] + jnp.einsum(
            "hqk,khd->qhd",
            expo_block.astype(jnp.bfloat16),
            value_heads,
            preferred_element_type=jnp.float32,
        )
        return (peak_new, total_new, weighted_new)

    initial = (
        jnp.full((head_count, query_rows), masked_score, jnp.float32),
        jnp.zeros((head_count, query_rows), jnp.float32),
        jnp.zeros((query_rows, head_count, HD), jnp.float32),
    )
    query_heads = queries.reshape(query_rows, head_count, HD)
    row_ids = jnp.arange(query_rows)
    diag_mask = row_ids[:, None] >= row_ids[None, :]
    pair_block = jnp.stack([keys, values])
    carried = attend(initial, query_heads, pair_block, diag_mask)
    for step_index in range(1, ctx_count):
        pair_block = from_behind(pair_block, CTX, 1)
        carried = attend(carried, query_heads, pair_block, ctx_where >= step_index)
    attended = (
        (carried[2] / carried[1].T[:, :, None])
        .astype(jnp.bfloat16)
        .reshape(query_rows, head_count * HD)
    )
    tok_count = residual.shape[0]
    term = jnp.dot(attended, out_proj, preferred_element_type=jnp.float32)
    exp_count = lax.axis_size("exp")
    group_terms = lax.all_to_all(
        term.astype(jnp.bfloat16).reshape(exp_count, query_rows // exp_count, term.shape[1]),
        "exp",
        split_axis=0,
        concat_axis=0,
        tiled=True,
    )
    mixed = jnp.sum(group_terms.astype(jnp.float32), axis=0)
    stream = residual.astype(jnp.float32) + mixed
    normed = (
        stream * lax.rsqrt(jnp.mean(stream * stream, axis=1, keepdims=True) + norm_eps) * norm_gain
    ).astype(jnp.bfloat16)
    width = normed.shape[1]
    per_token = routes.shape[1]
    experts = lax.axis_size("exp")
    capacity = min(tok_count, max(2, tok_count * per_token * 5 // (4 * experts)))
    pair_count = tok_count * per_token
    flat_routes = routes.reshape(pair_count)
    expert_hot = (flat_routes[:, None] == jnp.arange(experts)[None, :]).astype(jnp.int32)
    earlier = jnp.cumsum(expert_hot, axis=0) - expert_hot
    slot_index = jnp.sum(earlier * expert_hot, axis=1)
    position = flat_routes * capacity + slot_index
    position_hot = (position[:, None] == jnp.arange(experts * capacity)[None, :]).astype(
        jnp.float32
    )
    token_hot = (
        (jnp.arange(pair_count) // per_token)[:, None] == jnp.arange(tok_count)[None, :]
    ).astype(jnp.float32)
    pick_rows = jnp.einsum("pr,pt->rt", position_hot, token_hot).astype(jnp.bfloat16)
    outgoing = (
        jnp.dot(pick_rows, normed, preferred_element_type=jnp.float32)
        .astype(jnp.bfloat16)
        .reshape(experts, 8, capacity * width // 8)
    )
    received = lax.all_to_all(outgoing, "exp", split_axis=0, concat_axis=0, tiled=True)
    def gather_quarters(local, axis):
        across = lax.ppermute(local, "ctx_hi", [(0, 1), (1, 0)])
        pair = jnp.concatenate([local, across], axis=axis)
        return lax.all_gather(pair, "ctx_lo", axis=axis, tiled=True)

    gate_full = gather_quarters(w_gate[0], 1)
    up_full = gather_quarters(w_up[0], 1)
    down_full = gather_quarters(w_down[0], 0)
    rows = received.reshape(experts * capacity, width)
    gate = jnp.dot(rows, gate_full, preferred_element_type=jnp.float32)
    upper = jnp.dot(rows, up_full, preferred_element_type=jnp.float32)
    act_all = (jax.nn.silu(gate) * upper).astype(jnp.bfloat16)
    quarter = w_down.shape[1]
    quarter_terms = jnp.einsum(
        "rqf,qfd->qrd",
        act_all.reshape(experts * capacity, ctx_count, quarter),
        down_full.reshape(ctx_count, quarter, width),
        preferred_element_type=jnp.float32,
    ).astype(jnp.bfloat16)
    expert_out = (
        jnp.sum(quarter_terms.astype(jnp.float32), axis=0)
        .astype(jnp.bfloat16)
        .reshape(experts, 8, capacity * width // 8)
    )
    returned = lax.all_to_all(expert_out, "exp", split_axis=0, concat_axis=0, tiled=True)
    weigh_rows = jnp.einsum(
        "pr,pt->tr", position_hot, token_hot * combine.reshape(pair_count)[:, None]
    )
    moe_sum = jnp.dot(
        weigh_rows,
        returned.reshape(experts * capacity, width).astype(jnp.float32),
        precision=lax.Precision.HIGHEST,
    )
    return (stream + moe_sum).astype(jnp.bfloat16)


def solution(mesh):
    in_specs = (
        P(CTX, "exp"),
        P(CTX, "exp"),
        P(CTX, "exp"),
        P("exp", None),
        P((*CTX, "exp"), None),
        P(),
        P((*CTX, "exp"), None),
        P((*CTX, "exp"), None),
        P("exp", None, CTX),
        P("exp", None, CTX),
        P("exp", CTX, None),
    )
    out_specs = P((*CTX, "exp"), None)
    split_mesh = Mesh(mesh.devices.reshape(2, 2, -1), (*CTX, "exp"))
    return jax.shard_map(
        per_device, mesh=split_mesh, in_specs=in_specs, out_specs=out_specs, check_vma=False
    )
```

```python
import math

import jax
import jax.numpy as jnp
from jax import lax
from jax.sharding import PartitionSpec as P

HD = 128


masked_score = -1e30
norm_eps = 1e-06


def from_behind(shard, axis, by):
    peers = lax.axis_size(axis)
    pairs = [(i, i + by) for i in range(peers) if 0 <= i + by < peers]
    return lax.ppermute(shard, axis, pairs)


def per_device(
    queries, keys, values, out_proj, residual, norm_gain, routes, combine, w_gate, w_up, w_down
):
    query_rows = queries.shape[0]
    head_count = queries.shape[1] // HD
    scaling = 1.0 / math.sqrt(HD)
    ctx_where = lax.axis_index("ctx")
    ctx_count = lax.axis_size("ctx")

    def attend(carried, query_heads, pair_block, visible):
        key_count = pair_block.shape[1]
        key_heads = pair_block[0].reshape(key_count, head_count, HD)
        value_heads = pair_block[1].reshape(key_count, head_count, HD)
        scores = (
            jnp.einsum("qhd,khd->hqk", query_heads, key_heads, preferred_element_type=jnp.float32)
            * scaling
        )
        scores = jnp.where(visible, scores, masked_score)
        peak_old, total_old, weighted_old = carried
        peak_new = jnp.maximum(peak_old, jnp.max(scores, axis=2))
        expo_block = jnp.exp(scores - peak_new[:, :, None])
        factor = jnp.exp(peak_old - peak_new)
        total_new = total_old * factor + jnp.sum(expo_block, axis=2)
        weighted_new = weighted_old * factor.T[:, :, None] + jnp.einsum(
            "hqk,khd->qhd",
            expo_block.astype(jnp.bfloat16),
            value_heads,
            preferred_element_type=jnp.float32,
        )
        return (peak_new, total_new, weighted_new)

    initial = (
        jnp.full((head_count, query_rows), masked_score, jnp.float32),
        jnp.zeros((head_count, query_rows), jnp.float32),
        jnp.zeros((query_rows, head_count, HD), jnp.float32),
    )
    query_heads = queries.reshape(query_rows, head_count, HD)
    row_ids = jnp.arange(query_rows)
    diag_mask = row_ids[:, None] >= row_ids[None, :]
    pair_block = jnp.stack([keys, values])
    carried = attend(initial, query_heads, pair_block, diag_mask)
    for step_index in range(1, ctx_count):
        pair_block = from_behind(pair_block, "ctx", 1)
        carried = attend(carried, query_heads, pair_block, ctx_where >= step_index)
    gate_local, up_local, down_local, _ = lax.optimization_barrier(
        (w_gate[0], w_up[0], w_down[0], pair_block)
    )
    attended = (
        (carried[2] / carried[1].T[:, :, None])
        .astype(jnp.bfloat16)
        .reshape(query_rows, head_count * HD)
    )
    tok_count = residual.shape[0]
    term = jnp.dot(attended, out_proj, preferred_element_type=jnp.float32)
    exp_count = lax.axis_size("exp")
    group_terms = lax.all_to_all(
        term.astype(jnp.bfloat16).reshape(exp_count, query_rows // exp_count, term.shape[1]),
        "exp",
        split_axis=0,
        concat_axis=0,
        tiled=True,
    )
    mixed = jnp.sum(group_terms.astype(jnp.float32), axis=0)
    stream = residual.astype(jnp.float32) + mixed
    normed = (
        stream * lax.rsqrt(jnp.mean(stream * stream, axis=1, keepdims=True) + norm_eps) * norm_gain
    ).astype(jnp.bfloat16)
    width = normed.shape[1]
    per_token = routes.shape[1]
    experts = lax.axis_size("exp")
    capacity = min(tok_count, max(2, tok_count * per_token * 5 // (4 * experts)))
    pair_count = tok_count * per_token
    flat_routes = routes.reshape(pair_count)
    expert_hot = (flat_routes[:, None] == jnp.arange(experts)[None, :]).astype(jnp.int32)
    earlier = jnp.cumsum(expert_hot, axis=0) - expert_hot
    slot_index = jnp.sum(earlier * expert_hot, axis=1)
    position = flat_routes * capacity + slot_index
    position_hot = (position[:, None] == jnp.arange(experts * capacity)[None, :]).astype(
        jnp.float32
    )
    token_hot = (
        (jnp.arange(pair_count) // per_token)[:, None] == jnp.arange(tok_count)[None, :]
    ).astype(jnp.float32)
    pick_rows = jnp.einsum("pr,pt->rt", position_hot, token_hot).astype(jnp.bfloat16)
    outgoing = (
        jnp.dot(pick_rows, normed, preferred_element_type=jnp.float32)
        .astype(jnp.bfloat16)
        .reshape(experts, 8, capacity * width // 8)
    )
    received = lax.all_to_all(outgoing, "exp", split_axis=0, concat_axis=0, tiled=True)
    gate_full = lax.all_gather(gate_local, "ctx", axis=1, tiled=True)
    up_full = lax.all_gather(up_local, "ctx", axis=1, tiled=True)
    down_full = lax.all_gather(down_local, "ctx", axis=0, tiled=True)
    rows = received.reshape(experts * capacity, width)
    gate = jnp.dot(rows, gate_full, preferred_element_type=jnp.float32)
    upper = jnp.dot(rows, up_full, preferred_element_type=jnp.float32)
    act_all = (jax.nn.silu(gate) * upper).astype(jnp.bfloat16)
    quarter = w_down.shape[1]
    quarter_terms = jnp.einsum(
        "rqf,qfd->qrd",
        act_all.reshape(experts * capacity, ctx_count, quarter),
        down_full.reshape(ctx_count, quarter, width),
        preferred_element_type=jnp.float32,
    ).astype(jnp.bfloat16)
    expert_out = (
        jnp.sum(quarter_terms.astype(jnp.float32), axis=0)
        .astype(jnp.bfloat16)
        .reshape(experts, 8, capacity * width // 8)
    )
    returned = lax.all_to_all(expert_out, "exp", split_axis=0, concat_axis=0, tiled=True)
    weigh_rows = jnp.einsum(
        "pr,pt->tr", position_hot, token_hot * combine.reshape(pair_count)[:, None]
    )
    moe_sum = jnp.dot(
        weigh_rows,
        returned.reshape(experts * capacity, width).astype(jnp.float32),
        precision=lax.Precision.HIGHEST,
    )
    return (stream + moe_sum).astype(jnp.bfloat16)


def solution(mesh):
    in_specs = (
        P("ctx", "exp"),
        P("ctx", "exp"),
        P("ctx", "exp"),
        P("exp", None),
        P(("ctx", "exp"), None),
        P(),
        P(("ctx", "exp"), None),
        P(("ctx", "exp"), None),
        P("exp", None, "ctx"),
        P("exp", None, "ctx"),
        P("exp", "ctx", None),
    )
    out_specs = P(("ctx", "exp"), None)
    return jax.shard_map(
        per_device, mesh=mesh, in_specs=in_specs, out_specs=out_specs, check_vma=False
    )
```

```python
import math

import jax
import jax.numpy as jnp
from jax import lax
from jax.sharding import Mesh, PartitionSpec as P

HD = 128


EXP = ("exp_hi", "exp_lo")

masked_score = -1e30
norm_eps = 1e-06


def from_behind(shard, axis, by):
    peers = lax.axis_size(axis)
    pairs = [(i, i + by) for i in range(peers) if 0 <= i + by < peers]
    return lax.ppermute(shard, axis, pairs)


def per_device(
    queries, keys, values, out_proj, residual, norm_gain, routes, combine, w_gate, w_up, w_down
):
    query_rows = queries.shape[0]
    head_count = queries.shape[1] // HD
    scaling = 1.0 / math.sqrt(HD)
    ctx_where = lax.axis_index("ctx")
    ctx_count = lax.axis_size("ctx")

    def attend(carried, query_heads, pair_block, visible):
        key_count = pair_block.shape[1]
        key_heads = pair_block[0].reshape(key_count, head_count, HD)
        value_heads = pair_block[1].reshape(key_count, head_count, HD)
        scores = (
            jnp.einsum("qhd,khd->hqk", query_heads, key_heads, preferred_element_type=jnp.float32)
            * scaling
        )
        scores = jnp.where(visible, scores, masked_score)
        peak_old, total_old, weighted_old = carried
        peak_new = jnp.maximum(peak_old, jnp.max(scores, axis=2))
        expo_block = jnp.exp(scores - peak_new[:, :, None])
        factor = jnp.exp(peak_old - peak_new)
        total_new = total_old * factor + jnp.sum(expo_block, axis=2)
        weighted_new = weighted_old * factor.T[:, :, None] + jnp.einsum(
            "hqk,khd->qhd",
            expo_block.astype(jnp.bfloat16),
            value_heads,
            preferred_element_type=jnp.float32,
        )
        return (peak_new, total_new, weighted_new)

    initial = (
        jnp.full((head_count, query_rows), masked_score, jnp.float32),
        jnp.zeros((head_count, query_rows), jnp.float32),
        jnp.zeros((query_rows, head_count, HD), jnp.float32),
    )
    query_heads = queries.reshape(query_rows, head_count, HD)
    row_ids = jnp.arange(query_rows)
    diag_mask = row_ids[:, None] >= row_ids[None, :]
    pair_block = jnp.stack([keys, values])
    carried = attend(initial, query_heads, pair_block, diag_mask)
    for step_index in range(1, ctx_count):
        pair_block = from_behind(pair_block, "ctx", 1)
        carried = attend(carried, query_heads, pair_block, ctx_where >= step_index)
    attended = (
        (carried[2] / carried[1].T[:, :, None])
        .astype(jnp.bfloat16)
        .reshape(query_rows, head_count * HD)
    )
    tok_count = residual.shape[0]
    swap = [(0, 1), (1, 0)]
    lo_where = lax.axis_index("exp_lo")
    hi_count = lax.axis_size("exp_hi")
    partner_proj = lax.ppermute(out_proj, "exp_lo", swap)
    per_owner = query_rows // (hi_count * 2)
    by_owner = attended.reshape(hi_count, 2, per_owner, head_count * HD)
    mine = lax.dynamic_index_in_dim(by_owner, lo_where, axis=1, keepdims=False)
    theirs = lax.ppermute(
        lax.dynamic_index_in_dim(by_owner, 1 - lo_where, axis=1, keepdims=False), "exp_lo", swap
    )
    half_rows = hi_count * per_owner
    own_term = jnp.dot(
        mine.reshape(half_rows, head_count * HD), out_proj, preferred_element_type=jnp.float32
    ).astype(jnp.bfloat16)
    partner_term = jnp.dot(
        theirs.reshape(half_rows, head_count * HD), partner_proj, preferred_element_type=jnp.float32
    ).astype(jnp.bfloat16)
    pair_term = (own_term.astype(jnp.float32) + partner_term.astype(jnp.float32)).astype(jnp.bfloat16)
    group_terms = lax.all_to_all(
        pair_term.reshape(hi_count, per_owner, pair_term.shape[1]),
        "exp_hi",
        split_axis=0,
        concat_axis=0,
        tiled=True,
    )
    mixed = jnp.sum(group_terms.astype(jnp.float32), axis=0)
    stream = residual.astype(jnp.float32) + mixed
    normed = (
        stream * lax.rsqrt(jnp.mean(stream * stream, axis=1, keepdims=True) + norm_eps) * norm_gain
    ).astype(jnp.bfloat16)
    width = normed.shape[1]
    per_token = routes.shape[1]
    experts = lax.axis_size(EXP)
    capacity = min(tok_count, max(2, tok_count * per_token * 5 // (4 * experts)))
    pair_count = tok_count * per_token
    flat_routes = routes.reshape(pair_count)
    expert_hot = (flat_routes[:, None] == jnp.arange(experts)[None, :]).astype(jnp.int32)
    earlier = jnp.cumsum(expert_hot, axis=0) - expert_hot
    slot_index = jnp.sum(earlier * expert_hot, axis=1)
    position = flat_routes * capacity + slot_index
    position_hot = (position[:, None] == jnp.arange(experts * capacity)[None, :]).astype(
        jnp.float32
    )
    token_hot = (
        (jnp.arange(pair_count) // per_token)[:, None] == jnp.arange(tok_count)[None, :]
    ).astype(jnp.float32)
    pick_rows = jnp.einsum("pr,pt->rt", position_hot, token_hot).astype(jnp.bfloat16)
    outgoing = (
        jnp.dot(pick_rows, normed, preferred_element_type=jnp.float32)
        .astype(jnp.bfloat16)
        .reshape(experts, 8, capacity * width // 8)
    )
    received = lax.all_to_all(outgoing, EXP, split_axis=0, concat_axis=0, tiled=True)
    gate_full = lax.all_gather(w_gate[0], "ctx", axis=1, tiled=True)
    up_full = lax.all_gather(w_up[0], "ctx", axis=1, tiled=True)
    down_full = lax.all_gather(w_down[0], "ctx", axis=0, tiled=True)
    rows = received.reshape(experts * capacity, width)
    gate = jnp.dot(rows, gate_full, preferred_element_type=jnp.float32)
    upper = jnp.dot(rows, up_full, preferred_element_type=jnp.float32)
    act_all = (jax.nn.silu(gate) * upper).astype(jnp.bfloat16)
    quarter = w_down.shape[1]
    quarter_terms = jnp.einsum(
        "rqf,qfd->qrd",
        act_all.reshape(experts * capacity, ctx_count, quarter),
        down_full.reshape(ctx_count, quarter, width),
        preferred_element_type=jnp.float32,
    ).astype(jnp.bfloat16)
    expert_out = (
        jnp.sum(quarter_terms.astype(jnp.float32), axis=0)
        .astype(jnp.bfloat16)
        .reshape(experts, 8, capacity * width // 8)
    )
    returned = lax.all_to_all(expert_out, EXP, split_axis=0, concat_axis=0, tiled=True)
    weigh_rows = jnp.einsum(
        "pr,pt->tr", position_hot, token_hot * combine.reshape(pair_count)[:, None]
    )
    moe_sum = jnp.dot(
        weigh_rows,
        returned.reshape(experts * capacity, width).astype(jnp.float32),
        precision=lax.Precision.HIGHEST,
    )
    return (stream + moe_sum).astype(jnp.bfloat16)


def solution(mesh):
    in_specs = (
        P("ctx", EXP),
        P("ctx", EXP),
        P("ctx", EXP),
        P(EXP, None),
        P(("ctx", *EXP), None),
        P(),
        P(("ctx", *EXP), None),
        P(("ctx", *EXP), None),
        P(EXP, None, "ctx"),
        P(EXP, None, "ctx"),
        P(EXP, "ctx", None),
    )
    out_specs = P(("ctx", *EXP), None)
    split_mesh = Mesh(mesh.devices.reshape(mesh.devices.shape[0], -1, 2), ("ctx", *EXP))
    return jax.shard_map(
        per_device, mesh=split_mesh, in_specs=in_specs, out_specs=out_specs, check_vma=False
    )
```

```python
import math

import jax
import jax.numpy as jnp
from jax import lax
from jax.sharding import Mesh, PartitionSpec as P

HD = 128


EXP = ("exp_hi", "exp_lo")

masked_score = -1e30
norm_eps = 1e-06


def from_behind(shard, axis, by):
    peers = lax.axis_size(axis)
    pairs = [(i, i + by) for i in range(peers) if 0 <= i + by < peers]
    return lax.ppermute(shard, axis, pairs)


def per_device(
    queries, keys, values, out_proj, residual, norm_gain, routes, combine, w_gate, w_up, w_down
):
    query_rows = queries.shape[0]
    head_count = queries.shape[1] // HD
    scaling = 1.0 / math.sqrt(HD)
    ctx_where = lax.axis_index("ctx")
    ctx_count = lax.axis_size("ctx")

    def attend(carried, query_heads, pair_block, visible):
        key_count = pair_block.shape[1]
        key_heads = pair_block[0].reshape(key_count, head_count, HD)
        value_heads = pair_block[1].reshape(key_count, head_count, HD)
        scores = (
            jnp.einsum("qhd,khd->hqk", query_heads, key_heads, preferred_element_type=jnp.float32)
            * scaling
        )
        scores = jnp.where(visible, scores, masked_score)
        peak_old, total_old, weighted_old = carried
        peak_new = jnp.maximum(peak_old, jnp.max(scores, axis=2))
        expo_block = jnp.exp(scores - peak_new[:, :, None])
        factor = jnp.exp(peak_old - peak_new)
        total_new = total_old * factor + jnp.sum(expo_block, axis=2)
        weighted_new = weighted_old * factor.T[:, :, None] + jnp.einsum(
            "hqk,khd->qhd",
            expo_block.astype(jnp.bfloat16),
            value_heads,
            preferred_element_type=jnp.float32,
        )
        return (peak_new, total_new, weighted_new)

    initial = (
        jnp.full((head_count, query_rows), masked_score, jnp.float32),
        jnp.zeros((head_count, query_rows), jnp.float32),
        jnp.zeros((query_rows, head_count, HD), jnp.float32),
    )
    query_heads = queries.reshape(query_rows, head_count, HD)
    row_ids = jnp.arange(query_rows)
    diag_mask = row_ids[:, None] >= row_ids[None, :]
    pair_block = jnp.stack([keys, values])
    carried = attend(initial, query_heads, pair_block, diag_mask)
    for step_index in range(1, ctx_count):
        pair_block = from_behind(pair_block, "ctx", 1)
        carried = attend(carried, query_heads, pair_block, ctx_where >= step_index)
    gate_local, up_local, down_local, _ = lax.optimization_barrier(
        (w_gate[0], w_up[0], w_down[0], pair_block)
    )
    attended = (
        (carried[2] / carried[1].T[:, :, None])
        .astype(jnp.bfloat16)
        .reshape(query_rows, head_count * HD)
    )
    tok_count = residual.shape[0]
    swap = [(0, 1), (1, 0)]
    lo_where = lax.axis_index("exp_lo")
    hi_count = lax.axis_size("exp_hi")
    partner_proj = lax.ppermute(out_proj, "exp_lo", swap)
    per_owner = query_rows // (hi_count * 2)
    by_owner = attended.reshape(hi_count, 2, per_owner, head_count * HD)
    mine = lax.dynamic_index_in_dim(by_owner, lo_where, axis=1, keepdims=False)
    theirs = lax.ppermute(
        lax.dynamic_index_in_dim(by_owner, 1 - lo_where, axis=1, keepdims=False), "exp_lo", swap
    )
    half_rows = hi_count * per_owner
    own_term = jnp.dot(
        mine.reshape(half_rows, head_count * HD), out_proj, preferred_element_type=jnp.float32
    ).astype(jnp.bfloat16)
    partner_term = jnp.dot(
        theirs.reshape(half_rows, head_count * HD), partner_proj, preferred_element_type=jnp.float32
    ).astype(jnp.bfloat16)
    pair_term = (own_term.astype(jnp.float32) + partner_term.astype(jnp.float32)).astype(jnp.bfloat16)
    group_terms = lax.all_to_all(
        pair_term.reshape(hi_count, per_owner, pair_term.shape[1]),
        "exp_hi",
        split_axis=0,
        concat_axis=0,
        tiled=True,
    )
    mixed = jnp.sum(group_terms.astype(jnp.float32), axis=0)
    stream = residual.astype(jnp.float32) + mixed
    normed = (
        stream * lax.rsqrt(jnp.mean(stream * stream, axis=1, keepdims=True) + norm_eps) * norm_gain
    ).astype(jnp.bfloat16)
    width = normed.shape[1]
    per_token = routes.shape[1]
    experts = lax.axis_size(EXP)
    capacity = min(tok_count, max(2, tok_count * per_token * 5 // (4 * experts)))
    pair_count = tok_count * per_token
    flat_routes = routes.reshape(pair_count)
    expert_hot = (flat_routes[:, None] == jnp.arange(experts)[None, :]).astype(jnp.int32)
    earlier = jnp.cumsum(expert_hot, axis=0) - expert_hot
    slot_index = jnp.sum(earlier * expert_hot, axis=1)
    position = flat_routes * capacity + slot_index
    position_hot = (position[:, None] == jnp.arange(experts * capacity)[None, :]).astype(
        jnp.float32
    )
    token_hot = (
        (jnp.arange(pair_count) // per_token)[:, None] == jnp.arange(tok_count)[None, :]
    ).astype(jnp.float32)
    pick_rows = jnp.einsum("pr,pt->rt", position_hot, token_hot).astype(jnp.bfloat16)
    outgoing = (
        jnp.dot(pick_rows, normed, preferred_element_type=jnp.float32)
        .astype(jnp.bfloat16)
        .reshape(experts, 8, capacity * width // 8)
    )
    received = lax.all_to_all(outgoing, EXP, split_axis=0, concat_axis=0, tiled=True)
    gate_full = lax.all_gather(gate_local, "ctx", axis=1, tiled=True)
    up_full = lax.all_gather(up_local, "ctx", axis=1, tiled=True)
    down_full = lax.all_gather(down_local, "ctx", axis=0, tiled=True)
    rows = received.reshape(experts * capacity, width)
    gate = jnp.dot(rows, gate_full, preferred_element_type=jnp.float32)
    upper = jnp.dot(rows, up_full, preferred_element_type=jnp.float32)
    act_all = (jax.nn.silu(gate) * upper).astype(jnp.bfloat16)
    quarter = w_down.shape[1]
    quarter_terms = jnp.einsum(
        "rqf,qfd->qrd",
        act_all.reshape(experts * capacity, ctx_count, quarter),
        down_full.reshape(ctx_count, quarter, width),
        preferred_element_type=jnp.float32,
    ).astype(jnp.bfloat16)
    expert_out = (
        jnp.sum(quarter_terms.astype(jnp.float32), axis=0)
        .astype(jnp.bfloat16)
        .reshape(experts, 8, capacity * width // 8)
    )
    returned = lax.all_to_all(expert_out, EXP, split_axis=0, concat_axis=0, tiled=True)
    weigh_rows = jnp.einsum(
        "pr,pt->tr", position_hot, token_hot * combine.reshape(pair_count)[:, None]
    )
    moe_sum = jnp.dot(
        weigh_rows,
        returned.reshape(experts * capacity, width).astype(jnp.float32),
        precision=lax.Precision.HIGHEST,
    )
    return (stream + moe_sum).astype(jnp.bfloat16)


def solution(mesh):
    in_specs = (
        P("ctx", EXP),
        P("ctx", EXP),
        P("ctx", EXP),
        P(EXP, None),
        P(("ctx", *EXP), None),
        P(),
        P(("ctx", *EXP), None),
        P(("ctx", *EXP), None),
        P(EXP, None, "ctx"),
        P(EXP, None, "ctx"),
        P(EXP, "ctx", None),
    )
    out_specs = P(("ctx", *EXP), None)
    split_mesh = Mesh(mesh.devices.reshape(mesh.devices.shape[0], -1, 2), ("ctx", *EXP))
    return jax.shard_map(
        per_device, mesh=split_mesh, in_specs=in_specs, out_specs=out_specs, check_vma=False
    )
```

```python
import math

import jax
import jax.numpy as jnp
from jax import lax
from jax.sharding import Mesh, PartitionSpec as P

HD = 128


EXP = ("exp_hi", "exp_lo")
CTX = ("ctx_hi", "ctx_lo")

masked_score = -1e30
norm_eps = 1e-06


def from_behind(shard, axis, by):
    peers = lax.axis_size(axis)
    pairs = [(i, i + by) for i in range(peers) if 0 <= i + by < peers]
    return lax.ppermute(shard, axis, pairs)


def per_device(
    queries, keys, values, out_proj, residual, norm_gain, routes, combine, w_gate, w_up, w_down
):
    query_rows = queries.shape[0]
    head_count = queries.shape[1] // HD
    scaling = 1.0 / math.sqrt(HD)
    ctx_where = lax.axis_index(CTX)
    ctx_count = lax.axis_size(CTX)

    def attend(carried, query_heads, pair_block, visible):
        key_count = pair_block.shape[1]
        key_heads = pair_block[0].reshape(key_count, head_count, HD)
        value_heads = pair_block[1].reshape(key_count, head_count, HD)
        scores = (
            jnp.einsum("qhd,khd->hqk", query_heads, key_heads, preferred_element_type=jnp.float32)
            * scaling
        )
        scores = jnp.where(visible, scores, masked_score)
        peak_old, total_old, weighted_old = carried
        peak_new = jnp.maximum(peak_old, jnp.max(scores, axis=2))
        expo_block = jnp.exp(scores - peak_new[:, :, None])
        factor = jnp.exp(peak_old - peak_new)
        total_new = total_old * factor + jnp.sum(expo_block, axis=2)
        weighted_new = weighted_old * factor.T[:, :, None] + jnp.einsum(
            "hqk,khd->qhd",
            expo_block.astype(jnp.bfloat16),
            value_heads,
            preferred_element_type=jnp.float32,
        )
        return (peak_new, total_new, weighted_new)

    initial = (
        jnp.full((head_count, query_rows), masked_score, jnp.float32),
        jnp.zeros((head_count, query_rows), jnp.float32),
        jnp.zeros((query_rows, head_count, HD), jnp.float32),
    )
    query_heads = queries.reshape(query_rows, head_count, HD)
    row_ids = jnp.arange(query_rows)
    diag_mask = row_ids[:, None] >= row_ids[None, :]
    pair_block = jnp.stack([keys, values])
    carried = attend(initial, query_heads, pair_block, diag_mask)
    for step_index in range(1, ctx_count):
        pair_block = from_behind(pair_block, CTX, 1)
        carried = attend(carried, query_heads, pair_block, ctx_where >= step_index)
    gate_local, up_local, down_local, _ = lax.optimization_barrier(
        (w_gate[0], w_up[0], w_down[0], pair_block)
    )
    attended = (
        (carried[2] / carried[1].T[:, :, None])
        .astype(jnp.bfloat16)
        .reshape(query_rows, head_count * HD)
    )
    tok_count = residual.shape[0]
    swap = [(0, 1), (1, 0)]
    lo_where = lax.axis_index("exp_lo")
    hi_count = lax.axis_size("exp_hi")
    partner_proj = lax.ppermute(out_proj, "exp_lo", swap)
    per_owner = query_rows // (hi_count * 2)
    by_owner = attended.reshape(hi_count, 2, per_owner, head_count * HD)
    mine = lax.dynamic_index_in_dim(by_owner, lo_where, axis=1, keepdims=False)
    theirs = lax.ppermute(
        lax.dynamic_index_in_dim(by_owner, 1 - lo_where, axis=1, keepdims=False), "exp_lo", swap
    )
    half_rows = hi_count * per_owner
    own_term = jnp.dot(
        mine.reshape(half_rows, head_count * HD), out_proj, preferred_element_type=jnp.float32
    ).astype(jnp.bfloat16)
    partner_term = jnp.dot(
        theirs.reshape(half_rows, head_count * HD), partner_proj, preferred_element_type=jnp.float32
    ).astype(jnp.bfloat16)
    pair_term = (own_term.astype(jnp.float32) + partner_term.astype(jnp.float32)).astype(jnp.bfloat16)
    group_terms = lax.all_to_all(
        pair_term.reshape(hi_count, per_owner, pair_term.shape[1]),
        "exp_hi",
        split_axis=0,
        concat_axis=0,
        tiled=True,
    )
    mixed = jnp.sum(group_terms.astype(jnp.float32), axis=0)
    stream = residual.astype(jnp.float32) + mixed
    normed = (
        stream * lax.rsqrt(jnp.mean(stream * stream, axis=1, keepdims=True) + norm_eps) * norm_gain
    ).astype(jnp.bfloat16)
    width = normed.shape[1]
    per_token = routes.shape[1]
    experts = lax.axis_size(EXP)
    capacity = min(tok_count, max(2, tok_count * per_token * 5 // (4 * experts)))
    pair_count = tok_count * per_token
    flat_routes = routes.reshape(pair_count)
    expert_hot = (flat_routes[:, None] == jnp.arange(experts)[None, :]).astype(jnp.int32)
    earlier = jnp.cumsum(expert_hot, axis=0) - expert_hot
    slot_index = jnp.sum(earlier * expert_hot, axis=1)
    position = flat_routes * capacity + slot_index
    position_hot = (position[:, None] == jnp.arange(experts * capacity)[None, :]).astype(
        jnp.float32
    )
    token_hot = (
        (jnp.arange(pair_count) // per_token)[:, None] == jnp.arange(tok_count)[None, :]
    ).astype(jnp.float32)
    pick_rows = jnp.einsum("pr,pt->rt", position_hot, token_hot).astype(jnp.bfloat16)
    outgoing = (
        jnp.dot(pick_rows, normed, preferred_element_type=jnp.float32)
        .astype(jnp.bfloat16)
        .reshape(experts, 8, capacity * width // 8)
    )
    received = lax.all_to_all(outgoing, EXP, split_axis=0, concat_axis=0, tiled=True)
    def gather_quarters(local, axis):
        across = lax.ppermute(local, "ctx_hi", swap)
        pair = jnp.concatenate([local, across], axis=axis)
        return lax.all_gather(pair, "ctx_lo", axis=axis, tiled=True)

    gate_full = gather_quarters(gate_local, 1)
    up_full = gather_quarters(up_local, 1)
    down_full = gather_quarters(down_local, 0)
    rows = received.reshape(experts * capacity, width)
    gate = jnp.dot(rows, gate_full, preferred_element_type=jnp.float32)
    upper = jnp.dot(rows, up_full, preferred_element_type=jnp.float32)
    act_all = (jax.nn.silu(gate) * upper).astype(jnp.bfloat16)
    quarter = w_down.shape[1]
    quarter_terms = jnp.einsum(
        "rqf,qfd->qrd",
        act_all.reshape(experts * capacity, ctx_count, quarter),
        down_full.reshape(ctx_count, quarter, width),
        preferred_element_type=jnp.float32,
    ).astype(jnp.bfloat16)
    expert_out = (
        jnp.sum(quarter_terms.astype(jnp.float32), axis=0)
        .astype(jnp.bfloat16)
        .reshape(experts, 8, capacity * width // 8)
    )
    returned = lax.all_to_all(expert_out, EXP, split_axis=0, concat_axis=0, tiled=True)
    weigh_rows = jnp.einsum(
        "pr,pt->tr", position_hot, token_hot * combine.reshape(pair_count)[:, None]
    )
    moe_sum = jnp.dot(
        weigh_rows,
        returned.reshape(experts * capacity, width).astype(jnp.float32),
        precision=lax.Precision.HIGHEST,
    )
    return (stream + moe_sum).astype(jnp.bfloat16)


def solution(mesh):
    in_specs = (
        P(CTX, EXP),
        P(CTX, EXP),
        P(CTX, EXP),
        P(EXP, None),
        P((*CTX, *EXP), None),
        P(),
        P((*CTX, *EXP), None),
        P((*CTX, *EXP), None),
        P(EXP, None, CTX),
        P(EXP, None, CTX),
        P(EXP, CTX, None),
    )
    out_specs = P((*CTX, *EXP), None)
    split_mesh = Mesh(mesh.devices.reshape(2, -1, mesh.devices.shape[1] // 2, 2), (*CTX, *EXP))
    return jax.shard_map(
        per_device, mesh=split_mesh, in_specs=in_specs, out_specs=out_specs, check_vma=False
    )
```

```python
import math

import jax
import jax.numpy as jnp
from jax import lax
from jax.sharding import Mesh, PartitionSpec as P

HD = 128


EXP = ("exp_hi", "exp_lo")

masked_score = -1e30
norm_eps = 1e-06


def from_behind(shard, axis, by):
    peers = lax.axis_size(axis)
    pairs = [(i, i + by) for i in range(peers) if 0 <= i + by < peers]
    return lax.ppermute(shard, axis, pairs)


def per_device(
    queries, keys, values, out_proj, residual, norm_gain, routes, combine, w_gate, w_up, w_down
):
    query_rows = queries.shape[0]
    head_count = queries.shape[1] // HD
    scaling = 1.0 / math.sqrt(HD)
    ctx_where = lax.axis_index("ctx")
    ctx_count = lax.axis_size("ctx")

    def attend(carried, query_heads, pair_block, visible):
        key_count = pair_block.shape[1]
        key_heads = pair_block[0].reshape(key_count, head_count, HD)
        value_heads = pair_block[1].reshape(key_count, head_count, HD)
        scores = (
            jnp.einsum("qhd,khd->hqk", query_heads, key_heads, preferred_element_type=jnp.float32)
            * scaling
        )
        scores = jnp.where(visible, scores, masked_score)
        peak_old, total_old, weighted_old = carried
        peak_new = jnp.maximum(peak_old, jnp.max(scores, axis=2))
        expo_block = jnp.exp(scores - peak_new[:, :, None])
        factor = jnp.exp(peak_old - peak_new)
        total_new = total_old * factor + jnp.sum(expo_block, axis=2)
        weighted_new = weighted_old * factor.T[:, :, None] + jnp.einsum(
            "hqk,khd->qhd",
            expo_block.astype(jnp.bfloat16),
            value_heads,
            preferred_element_type=jnp.float32,
        )
        return (peak_new, total_new, weighted_new)

    initial = (
        jnp.full((head_count, query_rows), masked_score, jnp.float32),
        jnp.zeros((head_count, query_rows), jnp.float32),
        jnp.zeros((query_rows, head_count, HD), jnp.float32),
    )
    query_heads = queries.reshape(query_rows, head_count, HD)
    row_ids = jnp.arange(query_rows)
    diag_mask = row_ids[:, None] >= row_ids[None, :]
    pair_block = jnp.stack([keys, values])
    carried = attend(initial, query_heads, pair_block, diag_mask)
    for step_index in range(1, ctx_count):
        pair_block = from_behind(pair_block, "ctx", 1)
        carried = attend(carried, query_heads, pair_block, ctx_where >= step_index)
    gate_local = w_gate[0]
    up_local, down_local, _ = lax.optimization_barrier((w_up[0], w_down[0], pair_block))
    attended = (
        (carried[2] / carried[1].T[:, :, None])
        .astype(jnp.bfloat16)
        .reshape(query_rows, head_count * HD)
    )
    tok_count = residual.shape[0]
    swap = [(0, 1), (1, 0)]
    lo_where = lax.axis_index("exp_lo")
    hi_count = lax.axis_size("exp_hi")
    partner_proj = lax.ppermute(out_proj, "exp_lo", swap)
    per_owner = query_rows // (hi_count * 2)
    by_owner = attended.reshape(hi_count, 2, per_owner, head_count * HD)
    mine = lax.dynamic_index_in_dim(by_owner, lo_where, axis=1, keepdims=False)
    theirs = lax.ppermute(
        lax.dynamic_index_in_dim(by_owner, 1 - lo_where, axis=1, keepdims=False), "exp_lo", swap
    )
    half_rows = hi_count * per_owner
    own_term = jnp.dot(
        mine.reshape(half_rows, head_count * HD), out_proj, preferred_element_type=jnp.float32
    ).astype(jnp.bfloat16)
    partner_term = jnp.dot(
        theirs.reshape(half_rows, head_count * HD), partner_proj, preferred_element_type=jnp.float32
    ).astype(jnp.bfloat16)
    pair_term = (own_term.astype(jnp.float32) + partner_term.astype(jnp.float32)).astype(jnp.bfloat16)
    group_terms = lax.all_to_all(
        pair_term.reshape(hi_count, per_owner, pair_term.shape[1]),
        "exp_hi",
        split_axis=0,
        concat_axis=0,
        tiled=True,
    )
    mixed = jnp.sum(group_terms.astype(jnp.float32), axis=0)
    stream = residual.astype(jnp.float32) + mixed
    normed = (
        stream * lax.rsqrt(jnp.mean(stream * stream, axis=1, keepdims=True) + norm_eps) * norm_gain
    ).astype(jnp.bfloat16)
    width = normed.shape[1]
    per_token = routes.shape[1]
    experts = lax.axis_size(EXP)
    capacity = min(tok_count, max(2, tok_count * per_token * 5 // (4 * experts)))
    pair_count = tok_count * per_token
    flat_routes = routes.reshape(pair_count)
    expert_hot = (flat_routes[:, None] == jnp.arange(experts)[None, :]).astype(jnp.int32)
    earlier = jnp.cumsum(expert_hot, axis=0) - expert_hot
    slot_index = jnp.sum(earlier * expert_hot, axis=1)
    position = flat_routes * capacity + slot_index
    position_hot = (position[:, None] == jnp.arange(experts * capacity)[None, :]).astype(
        jnp.float32
    )
    token_hot = (
        (jnp.arange(pair_count) // per_token)[:, None] == jnp.arange(tok_count)[None, :]
    ).astype(jnp.float32)
    pick_rows = jnp.einsum("pr,pt->rt", position_hot, token_hot).astype(jnp.bfloat16)
    outgoing = (
        jnp.dot(pick_rows, normed, preferred_element_type=jnp.float32)
        .astype(jnp.bfloat16)
        .reshape(experts, 8, capacity * width // 8)
    )
    received = lax.all_to_all(outgoing, EXP, split_axis=0, concat_axis=0, tiled=True)
    gate_full = lax.all_gather(gate_local, "ctx", axis=1, tiled=True)
    up_full = lax.all_gather(up_local, "ctx", axis=1, tiled=True)
    down_full = lax.all_gather(down_local, "ctx", axis=0, tiled=True)
    rows = received.reshape(experts * capacity, width)
    gate = jnp.dot(rows, gate_full, preferred_element_type=jnp.float32)
    upper = jnp.dot(rows, up_full, preferred_element_type=jnp.float32)
    act_all = (jax.nn.silu(gate) * upper).astype(jnp.bfloat16)
    quarter = w_down.shape[1]
    quarter_terms = jnp.einsum(
        "rqf,qfd->qrd",
        act_all.reshape(experts * capacity, ctx_count, quarter),
        down_full.reshape(ctx_count, quarter, width),
        preferred_element_type=jnp.float32,
    ).astype(jnp.bfloat16)
    expert_out = (
        jnp.sum(quarter_terms.astype(jnp.float32), axis=0)
        .astype(jnp.bfloat16)
        .reshape(experts, 8, capacity * width // 8)
    )
    returned = lax.all_to_all(expert_out, EXP, split_axis=0, concat_axis=0, tiled=True)
    weigh_rows = jnp.einsum(
        "pr,pt->tr", position_hot, token_hot * combine.reshape(pair_count)[:, None]
    )
    moe_sum = jnp.dot(
        weigh_rows,
        returned.reshape(experts * capacity, width).astype(jnp.float32),
        precision=lax.Precision.HIGHEST,
    )
    return (stream + moe_sum).astype(jnp.bfloat16)


def solution(mesh):
    in_specs = (
        P("ctx", EXP),
        P("ctx", EXP),
        P("ctx", EXP),
        P(EXP, None),
        P(("ctx", *EXP), None),
        P(),
        P(("ctx", *EXP), None),
        P(("ctx", *EXP), None),
        P(EXP, None, "ctx"),
        P(EXP, None, "ctx"),
        P(EXP, "ctx", None),
    )
    out_specs = P(("ctx", *EXP), None)
    split_mesh = Mesh(mesh.devices.reshape(mesh.devices.shape[0], -1, 2), ("ctx", *EXP))
    return jax.shard_map(
        per_device, mesh=split_mesh, in_specs=in_specs, out_specs=out_specs, check_vma=False
    )
```

```python
import math

import jax
import jax.numpy as jnp
from jax import lax
from jax.sharding import Mesh, PartitionSpec as P

HD = 128


EXP = ("exp_hi", "exp_lo")

masked_score = -1e30
norm_eps = 1e-06


def from_behind(shard, axis, by):
    peers = lax.axis_size(axis)
    pairs = [(i, i + by) for i in range(peers) if 0 <= i + by < peers]
    return lax.ppermute(shard, axis, pairs)


def per_device(
    queries, keys, values, out_proj, residual, norm_gain, routes, combine, w_gate, w_up, w_down
):
    query_rows = queries.shape[0]
    head_count = queries.shape[1] // HD
    scaling = 1.0 / math.sqrt(HD)
    ctx_where = lax.axis_index("ctx")
    ctx_count = lax.axis_size("ctx")

    def attend(carried, query_heads, pair_block, visible):
        key_count = pair_block.shape[1]
        key_heads = pair_block[0].reshape(key_count, head_count, HD)
        value_heads = pair_block[1].reshape(key_count, head_count, HD)
        scores = (
            jnp.einsum("qhd,khd->hqk", query_heads, key_heads, preferred_element_type=jnp.float32)
            * scaling
        )
        scores = jnp.where(visible, scores, masked_score)
        peak_old, total_old, weighted_old = carried
        peak_new = jnp.maximum(peak_old, jnp.max(scores, axis=2))
        expo_block = jnp.exp(scores - peak_new[:, :, None])
        factor = jnp.exp(peak_old - peak_new)
        total_new = total_old * factor + jnp.sum(expo_block, axis=2)
        weighted_new = weighted_old * factor.T[:, :, None] + jnp.einsum(
            "hqk,khd->qhd",
            expo_block.astype(jnp.bfloat16),
            value_heads,
            preferred_element_type=jnp.float32,
        )
        return (peak_new, total_new, weighted_new)

    initial = (
        jnp.full((head_count, query_rows), masked_score, jnp.float32),
        jnp.zeros((head_count, query_rows), jnp.float32),
        jnp.zeros((query_rows, head_count, HD), jnp.float32),
    )
    query_heads = queries.reshape(query_rows, head_count, HD)
    row_ids = jnp.arange(query_rows)
    diag_mask = row_ids[:, None] >= row_ids[None, :]
    pair_block = jnp.stack([keys, values])
    carried = attend(initial, query_heads, pair_block, diag_mask)
    for step_index in range(1, ctx_count):
        pair_block = from_behind(pair_block, "ctx", 1)
        carried = attend(carried, query_heads, pair_block, ctx_where >= step_index)
    gate_local = w_gate[0]
    up_local, down_local, _ = lax.optimization_barrier((w_up[0], w_down[0], pair_block))
    attended = (
        (carried[2] / carried[1].T[:, :, None])
        .astype(jnp.bfloat16)
        .reshape(query_rows, head_count * HD)
    )
    tok_count = residual.shape[0]
    swap = [(0, 1), (1, 0)]
    lo_where = lax.axis_index("exp_lo")
    hi_count = lax.axis_size("exp_hi")
    partner_proj = lax.ppermute(out_proj, "exp_lo", swap)
    per_owner = query_rows // (hi_count * 2)
    by_owner = attended.reshape(hi_count, 2, per_owner, head_count * HD)
    mine = lax.dynamic_index_in_dim(by_owner, lo_where, axis=1, keepdims=False)
    theirs = lax.ppermute(
        lax.dynamic_index_in_dim(by_owner, 1 - lo_where, axis=1, keepdims=False), "exp_lo", swap
    )
    half_rows = hi_count * per_owner
    own_term = jnp.dot(
        mine.reshape(half_rows, head_count * HD), out_proj, preferred_element_type=jnp.float32
    ).astype(jnp.bfloat16)
    partner_term = jnp.dot(
        theirs.reshape(half_rows, head_count * HD), partner_proj, preferred_element_type=jnp.float32
    ).astype(jnp.bfloat16)
    pair_term = (own_term.astype(jnp.float32) + partner_term.astype(jnp.float32)).astype(jnp.bfloat16)
    group_terms = lax.all_to_all(
        pair_term.reshape(hi_count, per_owner, pair_term.shape[1]),
        "exp_hi",
        split_axis=0,
        concat_axis=0,
        tiled=True,
    )
    mixed = jnp.sum(group_terms.astype(jnp.float32), axis=0)
    stream = residual.astype(jnp.float32) + mixed
    normed = (
        stream * lax.rsqrt(jnp.mean(stream * stream, axis=1, keepdims=True) + norm_eps) * norm_gain
    ).astype(jnp.bfloat16)
    width = normed.shape[1]
    per_token = routes.shape[1]
    experts = lax.axis_size(EXP)
    capacity = min(tok_count, max(2, tok_count * per_token * 5 // (4 * experts)))
    pair_count = tok_count * per_token
    flat_routes = routes.reshape(pair_count)
    expert_hot = (flat_routes[:, None] == jnp.arange(experts)[None, :]).astype(jnp.int32)
    earlier = jnp.cumsum(expert_hot, axis=0) - expert_hot
    slot_index = jnp.sum(earlier * expert_hot, axis=1)
    position = flat_routes * capacity + slot_index
    position_hot = (position[:, None] == jnp.arange(experts * capacity)[None, :]).astype(
        jnp.float32
    )
    token_hot = (
        (jnp.arange(pair_count) // per_token)[:, None] == jnp.arange(tok_count)[None, :]
    ).astype(jnp.float32)
    pick_rows = jnp.einsum("pr,pt->rt", position_hot, token_hot).astype(jnp.bfloat16)
    outgoing = (
        jnp.dot(pick_rows, normed, preferred_element_type=jnp.float32)
        .astype(jnp.bfloat16)
        .reshape(experts, 8, capacity * width // 8)
    )
    received = lax.all_to_all(outgoing, EXP, split_axis=0, concat_axis=0, tiled=True)
    gate_full = lax.all_gather(gate_local, "ctx", axis=1, tiled=True)
    up_full = lax.all_gather(up_local, "ctx", axis=1, tiled=True)
    down_pieces = [down_local] + [
        lax.ppermute(down_local, "ctx", [(i, (i + shift) % ctx_count) for i in range(ctx_count)])
        for shift in range(1, ctx_count)
    ]
    rows = received.reshape(experts * capacity, width)
    gate = jnp.dot(rows, gate_full, preferred_element_type=jnp.float32)
    upper = jnp.dot(rows, up_full, preferred_element_type=jnp.float32)
    act_all = (jax.nn.silu(gate) * upper).astype(jnp.bfloat16)
    quarter = w_down.shape[1]
    act_quarters = act_all.reshape(experts * capacity, ctx_count, quarter)
    expert_sum = jnp.zeros((experts * capacity, width), jnp.float32)
    for piece_index, piece in enumerate(down_pieces):
        act_piece = lax.dynamic_index_in_dim(
            act_quarters, (ctx_where - piece_index) % ctx_count, axis=1, keepdims=False
        )
        expert_sum = expert_sum + jnp.dot(
            act_piece, piece, preferred_element_type=jnp.float32
        ).astype(jnp.bfloat16).astype(jnp.float32)
    expert_out = (
        expert_sum.astype(jnp.bfloat16)
        .reshape(experts, 8, capacity * width // 8)
    )
    returned = lax.all_to_all(expert_out, EXP, split_axis=0, concat_axis=0, tiled=True)
    weigh_rows = jnp.einsum(
        "pr,pt->tr", position_hot, token_hot * combine.reshape(pair_count)[:, None]
    )
    moe_sum = jnp.dot(
        weigh_rows,
        returned.reshape(experts * capacity, width).astype(jnp.float32),
        precision=lax.Precision.HIGHEST,
    )
    return (stream + moe_sum).astype(jnp.bfloat16)


def solution(mesh):
    in_specs = (
        P("ctx", EXP),
        P("ctx", EXP),
        P("ctx", EXP),
        P(EXP, None),
        P(("ctx", *EXP), None),
        P(),
        P(("ctx", *EXP), None),
        P(("ctx", *EXP), None),
        P(EXP, None, "ctx"),
        P(EXP, None, "ctx"),
        P(EXP, "ctx", None),
    )
    out_specs = P(("ctx", *EXP), None)
    split_mesh = Mesh(mesh.devices.reshape(mesh.devices.shape[0], -1, 2), ("ctx", *EXP))
    return jax.shard_map(
        per_device, mesh=split_mesh, in_specs=in_specs, out_specs=out_specs, check_vma=False
    )
```

```python
import math

import jax
import jax.numpy as jnp
from jax import lax
from jax.sharding import Mesh, PartitionSpec as P

HD = 128


EXP = ("exp_hi", "exp_lo")

masked_score = -1e30
norm_eps = 1e-06


def from_behind(shard, axis, by):
    peers = lax.axis_size(axis)
    pairs = [(i, i + by) for i in range(peers) if 0 <= i + by < peers]
    return lax.ppermute(shard, axis, pairs)


def per_device(
    queries, keys, values, out_proj, residual, norm_gain, routes, combine, w_gate, w_up, w_down
):
    query_rows = queries.shape[0]
    head_count = queries.shape[1] // HD
    scaling = 1.0 / math.sqrt(HD)
    ctx_where = lax.axis_index("ctx")
    ctx_count = lax.axis_size("ctx")

    def attend(carried, query_heads, pair_block, visible):
        key_count = pair_block.shape[1]
        key_heads = pair_block[0].reshape(key_count, head_count, HD)
        value_heads = pair_block[1].reshape(key_count, head_count, HD)
        scores = (
            jnp.einsum("qhd,khd->hqk", query_heads, key_heads, preferred_element_type=jnp.float32)
            * scaling
        )
        scores = jnp.where(visible, scores, masked_score)
        peak_old, total_old, weighted_old = carried
        peak_new = jnp.maximum(peak_old, jnp.max(scores, axis=2))
        expo_block = jnp.exp(scores - peak_new[:, :, None])
        factor = jnp.exp(peak_old - peak_new)
        total_new = total_old * factor + jnp.sum(expo_block, axis=2)
        weighted_new = weighted_old * factor.T[:, :, None] + jnp.einsum(
            "hqk,khd->qhd",
            expo_block.astype(jnp.bfloat16),
            value_heads,
            preferred_element_type=jnp.float32,
        )
        return (peak_new, total_new, weighted_new)

    initial = (
        jnp.full((head_count, query_rows), masked_score, jnp.float32),
        jnp.zeros((head_count, query_rows), jnp.float32),
        jnp.zeros((query_rows, head_count, HD), jnp.float32),
    )
    query_heads = queries.reshape(query_rows, head_count, HD)
    row_ids = jnp.arange(query_rows)
    diag_mask = row_ids[:, None] >= row_ids[None, :]
    pair_block = jnp.stack([keys, values])
    carried = attend(initial, query_heads, pair_block, diag_mask)
    for step_index in range(1, ctx_count):
        pair_block = from_behind(pair_block, "ctx", 1)
        carried = attend(carried, query_heads, pair_block, ctx_where >= step_index)
    gate_local = w_gate[0]
    up_local, down_local, _ = lax.optimization_barrier((w_up[0], w_down[0], pair_block))
    attended = (
        (carried[2] / carried[1].T[:, :, None])
        .astype(jnp.bfloat16)
        .reshape(query_rows, head_count * HD)
    )
    tok_count = residual.shape[0]
    swap = [(0, 1), (1, 0)]
    lo_where = lax.axis_index("exp_lo")
    hi_count = lax.axis_size("exp_hi")
    partner_proj = lax.ppermute(out_proj, "exp_lo", swap)
    per_owner = query_rows // (hi_count * 2)
    by_owner = attended.reshape(hi_count, 2, per_owner, head_count * HD)
    mine = lax.dynamic_index_in_dim(by_owner, lo_where, axis=1, keepdims=False)
    theirs = lax.ppermute(
        lax.dynamic_index_in_dim(by_owner, 1 - lo_where, axis=1, keepdims=False), "exp_lo", swap
    )
    half_rows = hi_count * per_owner
    own_term = jnp.dot(
        mine.reshape(half_rows, head_count * HD), out_proj, preferred_element_type=jnp.float32
    ).astype(jnp.bfloat16)
    partner_term = jnp.dot(
        theirs.reshape(half_rows, head_count * HD), partner_proj, preferred_element_type=jnp.float32
    ).astype(jnp.bfloat16)
    pair_term = (own_term.astype(jnp.float32) + partner_term.astype(jnp.float32)).astype(jnp.bfloat16)
    group_terms = lax.all_to_all(
        pair_term.reshape(hi_count, per_owner, pair_term.shape[1]),
        "exp_hi",
        split_axis=0,
        concat_axis=0,
        tiled=True,
    )
    mixed = jnp.sum(group_terms.astype(jnp.float32), axis=0)
    stream = residual.astype(jnp.float32) + mixed
    normed = (
        stream * lax.rsqrt(jnp.mean(stream * stream, axis=1, keepdims=True) + norm_eps) * norm_gain
    ).astype(jnp.bfloat16)
    width = normed.shape[1]
    per_token = routes.shape[1]
    experts = lax.axis_size(EXP)
    capacity = min(tok_count, max(2, tok_count * per_token * 5 // (4 * experts)))
    pair_count = tok_count * per_token
    flat_routes = routes.reshape(pair_count)
    expert_hot = (flat_routes[:, None] == jnp.arange(experts)[None, :]).astype(jnp.int32)
    earlier = jnp.cumsum(expert_hot, axis=0) - expert_hot
    slot_index = jnp.sum(earlier * expert_hot, axis=1)
    position = flat_routes * capacity + slot_index
    position_hot = (position[:, None] == jnp.arange(experts * capacity)[None, :]).astype(
        jnp.float32
    )
    token_hot = (
        (jnp.arange(pair_count) // per_token)[:, None] == jnp.arange(tok_count)[None, :]
    ).astype(jnp.float32)
    pick_rows = jnp.einsum("pr,pt->rt", position_hot, token_hot).astype(jnp.bfloat16)
    outgoing = (
        jnp.dot(pick_rows, normed, preferred_element_type=jnp.float32)
        .astype(jnp.bfloat16)
        .reshape(experts, 8, capacity * width // 8)
    )
    received = lax.all_to_all(outgoing, EXP, split_axis=0, concat_axis=0, tiled=True)
    gate_full = lax.all_gather(gate_local, "ctx", axis=1, tiled=True)
    up_full = lax.all_gather(up_local, "ctx", axis=1, tiled=True)
    half_width = width // 2
    down_halves = [
        lax.all_gather(down_local[:, :half_width], "ctx", axis=0, tiled=True),
        lax.all_gather(down_local[:, half_width:], "ctx", axis=0, tiled=True),
    ]
    rows = received.reshape(experts * capacity, width)
    gate = jnp.dot(rows, gate_full, preferred_element_type=jnp.float32)
    upper = jnp.dot(rows, up_full, preferred_element_type=jnp.float32)
    act_all = (jax.nn.silu(gate) * upper).astype(jnp.bfloat16)
    quarter = w_down.shape[1]
    weigh_rows = jnp.einsum(
        "pr,pt->tr", position_hot, token_hot * combine.reshape(pair_count)[:, None]
    )
    moe_parts = []
    for down_half in down_halves:
        quarter_terms = jnp.einsum(
            "rqf,qfd->qrd",
            act_all.reshape(experts * capacity, ctx_count, quarter),
            down_half.reshape(ctx_count, quarter, half_width),
            preferred_element_type=jnp.float32,
        ).astype(jnp.bfloat16)
        expert_out = (
            jnp.sum(quarter_terms.astype(jnp.float32), axis=0)
            .astype(jnp.bfloat16)
            .reshape(experts, 8, capacity * half_width // 8)
        )
        returned = lax.all_to_all(expert_out, EXP, split_axis=0, concat_axis=0, tiled=True)
        moe_parts.append(
            jnp.dot(
                weigh_rows,
                returned.reshape(experts * capacity, half_width).astype(jnp.float32),
                precision=lax.Precision.HIGHEST,
            )
        )
    moe_sum = jnp.concatenate(moe_parts, axis=1)
    return (stream + moe_sum).astype(jnp.bfloat16)


def solution(mesh):
    in_specs = (
        P("ctx", EXP),
        P("ctx", EXP),
        P("ctx", EXP),
        P(EXP, None),
        P(("ctx", *EXP), None),
        P(),
        P(("ctx", *EXP), None),
        P(("ctx", *EXP), None),
        P(EXP, None, "ctx"),
        P(EXP, None, "ctx"),
        P(EXP, "ctx", None),
    )
    out_specs = P(("ctx", *EXP), None)
    split_mesh = Mesh(mesh.devices.reshape(mesh.devices.shape[0], -1, 2), ("ctx", *EXP))
    return jax.shard_map(
        per_device, mesh=split_mesh, in_specs=in_specs, out_specs=out_specs, check_vma=False
    )
```

```python
import math

import jax
import jax.numpy as jnp
from jax import lax
from jax.sharding import Mesh, PartitionSpec as P

HD = 128


EXP = ("exp_hi", "exp_lo")

masked_score = -1e30
norm_eps = 1e-06


def from_behind(shard, axis, by):
    peers = lax.axis_size(axis)
    pairs = [(i, i + by) for i in range(peers) if 0 <= i + by < peers]
    return lax.ppermute(shard, axis, pairs)


def per_device(
    queries, keys, values, out_proj, residual, norm_gain, routes, combine, w_gate, w_up, w_down
):
    query_rows = queries.shape[0]
    head_count = queries.shape[1] // HD
    scaling = 1.0 / math.sqrt(HD)
    ctx_where = lax.axis_index("ctx")
    ctx_count = lax.axis_size("ctx")

    def attend(carried, query_heads, pair_block, visible):
        key_count = pair_block.shape[1]
        key_heads = pair_block[0].reshape(key_count, head_count, HD)
        value_heads = pair_block[1].reshape(key_count, head_count, HD)
        scores = (
            jnp.einsum("qhd,khd->hqk", query_heads, key_heads, preferred_element_type=jnp.float32)
            * scaling
        )
        scores = jnp.where(visible, scores, masked_score)
        peak_old, total_old, weighted_old = carried
        peak_new = jnp.maximum(peak_old, jnp.max(scores, axis=2))
        expo_block = jnp.exp(scores - peak_new[:, :, None])
        factor = jnp.exp(peak_old - peak_new)
        total_new = total_old * factor + jnp.sum(expo_block, axis=2)
        weighted_new = weighted_old * factor.T[:, :, None] + jnp.einsum(
            "hqk,khd->qhd",
            expo_block.astype(jnp.bfloat16),
            value_heads,
            preferred_element_type=jnp.float32,
        )
        return (peak_new, total_new, weighted_new)

    initial = (
        jnp.full((head_count, query_rows), masked_score, jnp.float32),
        jnp.zeros((head_count, query_rows), jnp.float32),
        jnp.zeros((query_rows, head_count, HD), jnp.float32),
    )
    query_heads = queries.reshape(query_rows, head_count, HD)
    row_ids = jnp.arange(query_rows)
    diag_mask = row_ids[:, None] >= row_ids[None, :]
    pair_block = jnp.stack([keys, values])
    carried = attend(initial, query_heads, pair_block, diag_mask)
    for step_index in range(1, ctx_count):
        pair_block = from_behind(pair_block, "ctx", 1)
        carried = attend(carried, query_heads, pair_block, ctx_where >= step_index)
    gate_local = w_gate[0]
    up_local, down_local, _ = lax.optimization_barrier((w_up[0], w_down[0], pair_block))
    attended = (
        (carried[2] / carried[1].T[:, :, None])
        .astype(jnp.bfloat16)
        .reshape(query_rows, head_count * HD)
    )
    tok_count = residual.shape[0]
    swap = [(0, 1), (1, 0)]
    lo_where = lax.axis_index("exp_lo")
    hi_count = lax.axis_size("exp_hi")
    partner_proj = lax.ppermute(out_proj, "exp_lo", swap)
    per_owner = query_rows // (hi_count * 2)
    by_owner = attended.reshape(hi_count, 2, per_owner, head_count * HD)
    mine = lax.dynamic_index_in_dim(by_owner, lo_where, axis=1, keepdims=False)
    theirs = lax.ppermute(
        lax.dynamic_index_in_dim(by_owner, 1 - lo_where, axis=1, keepdims=False), "exp_lo", swap
    )
    half_rows = hi_count * per_owner
    own_term = jnp.dot(
        mine.reshape(half_rows, head_count * HD), out_proj, preferred_element_type=jnp.float32
    ).astype(jnp.bfloat16)
    partner_term = jnp.dot(
        theirs.reshape(half_rows, head_count * HD), partner_proj, preferred_element_type=jnp.float32
    ).astype(jnp.bfloat16)
    pair_term = (own_term.astype(jnp.float32) + partner_term.astype(jnp.float32)).astype(jnp.bfloat16)
    group_terms = lax.all_to_all(
        pair_term.reshape(hi_count, per_owner, pair_term.shape[1]),
        "exp_hi",
        split_axis=0,
        concat_axis=0,
        tiled=True,
    )
    mixed = jnp.sum(group_terms.astype(jnp.float32), axis=0)
    stream = residual.astype(jnp.float32) + mixed
    normed = (
        stream * lax.rsqrt(jnp.mean(stream * stream, axis=1, keepdims=True) + norm_eps) * norm_gain
    ).astype(jnp.bfloat16)
    width = normed.shape[1]
    per_token = routes.shape[1]
    experts = lax.axis_size(EXP)
    capacity = min(tok_count, max(2, tok_count * per_token * 5 // (4 * experts)))
    pair_count = tok_count * per_token
    flat_routes = routes.reshape(pair_count)
    expert_hot = (flat_routes[:, None] == jnp.arange(experts)[None, :]).astype(jnp.int32)
    earlier = jnp.cumsum(expert_hot, axis=0) - expert_hot
    slot_index = jnp.sum(earlier * expert_hot, axis=1)
    position = flat_routes * capacity + slot_index
    position_hot = (position[:, None] == jnp.arange(experts * capacity)[None, :]).astype(
        jnp.float32
    )
    token_hot = (
        (jnp.arange(pair_count) // per_token)[:, None] == jnp.arange(tok_count)[None, :]
    ).astype(jnp.float32)
    pick_rows = jnp.einsum("pr,pt->rt", position_hot, token_hot).astype(jnp.bfloat16)
    outgoing = (
        jnp.dot(pick_rows, normed, preferred_element_type=jnp.float32)
        .astype(jnp.bfloat16)
        .reshape(experts, 8, capacity * width // 8)
    )
    received = lax.all_to_all(outgoing, EXP, split_axis=0, concat_axis=0, tiled=True)
    gate_full = lax.all_gather(gate_local, "ctx", axis=1, tiled=True)
    up_down = lax.all_gather(
        jnp.stack([up_local, down_local.reshape(up_local.shape)]), "ctx", axis=0, tiled=False
    )
    up_full = jnp.concatenate(list(up_down[:, 0]), axis=1)
    down_full = up_down[:, 1].reshape(ctx_count * down_local.shape[0], down_local.shape[1])
    rows = received.reshape(experts * capacity, width)
    gate = jnp.dot(rows, gate_full, preferred_element_type=jnp.float32)
    upper = jnp.dot(rows, up_full, preferred_element_type=jnp.float32)
    act_all = (jax.nn.silu(gate) * upper).astype(jnp.bfloat16)
    quarter = w_down.shape[1]
    quarter_terms = jnp.einsum(
        "rqf,qfd->qrd",
        act_all.reshape(experts * capacity, ctx_count, quarter),
        down_full.reshape(ctx_count, quarter, width),
        preferred_element_type=jnp.float32,
    ).astype(jnp.bfloat16)
    expert_out = (
        jnp.sum(quarter_terms.astype(jnp.float32), axis=0)
        .astype(jnp.bfloat16)
        .reshape(experts, 8, capacity * width // 8)
    )
    returned = lax.all_to_all(expert_out, EXP, split_axis=0, concat_axis=0, tiled=True)
    weigh_rows = jnp.einsum(
        "pr,pt->tr", position_hot, token_hot * combine.reshape(pair_count)[:, None]
    )
    moe_sum = jnp.dot(
        weigh_rows,
        returned.reshape(experts * capacity, width).astype(jnp.float32),
        precision=lax.Precision.HIGHEST,
    )
    return (stream + moe_sum).astype(jnp.bfloat16)


def solution(mesh):
    in_specs = (
        P("ctx", EXP),
        P("ctx", EXP),
        P("ctx", EXP),
        P(EXP, None),
        P(("ctx", *EXP), None),
        P(),
        P(("ctx", *EXP), None),
        P(("ctx", *EXP), None),
        P(EXP, None, "ctx"),
        P(EXP, None, "ctx"),
        P(EXP, "ctx", None),
    )
    out_specs = P(("ctx", *EXP), None)
    split_mesh = Mesh(mesh.devices.reshape(mesh.devices.shape[0], -1, 2), ("ctx", *EXP))
    return jax.shard_map(
        per_device, mesh=split_mesh, in_specs=in_specs, out_specs=out_specs, check_vma=False
    )
```

```python
import math

import jax
import jax.numpy as jnp
from jax import lax
from jax.sharding import Mesh, PartitionSpec as P

HD = 128


EXP = ("exp_hi", "exp_lo")

masked_score = -1e30
norm_eps = 1e-06


def from_behind(shard, axis, by):
    peers = lax.axis_size(axis)
    pairs = [(i, i + by) for i in range(peers) if 0 <= i + by < peers]
    return lax.ppermute(shard, axis, pairs)


def per_device(
    queries, keys, values, out_proj, residual, norm_gain, routes, combine, w_gate, w_up, w_down
):
    query_rows = queries.shape[0]
    head_count = queries.shape[1] // HD
    scaling = 1.0 / math.sqrt(HD)
    ctx_where = lax.axis_index("ctx")
    ctx_count = lax.axis_size("ctx")

    def attend(carried, query_heads, pair_block, visible):
        key_count = pair_block.shape[1]
        key_heads = pair_block[0].reshape(key_count, head_count, HD)
        value_heads = pair_block[1].reshape(key_count, head_count, HD)
        scores = (
            jnp.einsum("qhd,khd->hqk", query_heads, key_heads, preferred_element_type=jnp.float32)
            * scaling
        )
        scores = jnp.where(visible, scores, masked_score)
        peak_old, total_old, weighted_old = carried
        peak_new = jnp.maximum(peak_old, jnp.max(scores, axis=2))
        expo_block = jnp.exp(scores - peak_new[:, :, None])
        factor = jnp.exp(peak_old - peak_new)
        total_new = total_old * factor + jnp.sum(expo_block, axis=2)
        weighted_new = weighted_old * factor.T[:, :, None] + jnp.einsum(
            "hqk,khd->qhd",
            expo_block.astype(jnp.bfloat16),
            value_heads,
            preferred_element_type=jnp.float32,
        )
        return (peak_new, total_new, weighted_new)

    initial = (
        jnp.full((head_count, query_rows), masked_score, jnp.float32),
        jnp.zeros((head_count, query_rows), jnp.float32),
        jnp.zeros((query_rows, head_count, HD), jnp.float32),
    )
    query_heads = queries.reshape(query_rows, head_count, HD)
    row_ids = jnp.arange(query_rows)
    diag_mask = row_ids[:, None] >= row_ids[None, :]
    pair_block = jnp.stack([keys, values])
    carried = attend(initial, query_heads, pair_block, diag_mask)
    for step_index in range(1, ctx_count):
        pair_block = from_behind(pair_block, "ctx", 1)
        carried = attend(carried, query_heads, pair_block, ctx_where >= step_index)
    gate_local = w_gate[0]
    up_local = w_up[0]
    down_local, _ = lax.optimization_barrier((w_down[0], pair_block))
    attended = (
        (carried[2] / carried[1].T[:, :, None])
        .astype(jnp.bfloat16)
        .reshape(query_rows, head_count * HD)
    )
    tok_count = residual.shape[0]
    swap = [(0, 1), (1, 0)]
    lo_where = lax.axis_index("exp_lo")
    hi_count = lax.axis_size("exp_hi")
    partner_proj = lax.ppermute(out_proj, "exp_lo", swap)
    per_owner = query_rows // (hi_count * 2)
    by_owner = attended.reshape(hi_count, 2, per_owner, head_count * HD)
    mine = lax.dynamic_index_in_dim(by_owner, lo_where, axis=1, keepdims=False)
    theirs = lax.ppermute(
        lax.dynamic_index_in_dim(by_owner, 1 - lo_where, axis=1, keepdims=False), "exp_lo", swap
    )
    half_rows = hi_count * per_owner
    own_term = jnp.dot(
        mine.reshape(half_rows, head_count * HD), out_proj, preferred_element_type=jnp.float32
    ).astype(jnp.bfloat16)
    partner_term = jnp.dot(
        theirs.reshape(half_rows, head_count * HD), partner_proj, preferred_element_type=jnp.float32
    ).astype(jnp.bfloat16)
    pair_term = (own_term.astype(jnp.float32) + partner_term.astype(jnp.float32)).astype(jnp.bfloat16)
    group_terms = lax.all_to_all(
        pair_term.reshape(hi_count, per_owner, pair_term.shape[1]),
        "exp_hi",
        split_axis=0,
        concat_axis=0,
        tiled=True,
    )
    mixed = jnp.sum(group_terms.astype(jnp.float32), axis=0)
    stream = residual.astype(jnp.float32) + mixed
    normed = (
        stream * lax.rsqrt(jnp.mean(stream * stream, axis=1, keepdims=True) + norm_eps) * norm_gain
    ).astype(jnp.bfloat16)
    width = normed.shape[1]
    per_token = routes.shape[1]
    experts = lax.axis_size(EXP)
    capacity = min(tok_count, max(2, tok_count * per_token * 5 // (4 * experts)))
    pair_count = tok_count * per_token
    flat_routes = routes.reshape(pair_count)
    expert_hot = (flat_routes[:, None] == jnp.arange(experts)[None, :]).astype(jnp.int32)
    earlier = jnp.cumsum(expert_hot, axis=0) - expert_hot
    slot_index = jnp.sum(earlier * expert_hot, axis=1)
    position = flat_routes * capacity + slot_index
    position_hot = (position[:, None] == jnp.arange(experts * capacity)[None, :]).astype(
        jnp.float32
    )
    token_hot = (
        (jnp.arange(pair_count) // per_token)[:, None] == jnp.arange(tok_count)[None, :]
    ).astype(jnp.float32)
    pick_rows = jnp.einsum("pr,pt->rt", position_hot, token_hot).astype(jnp.bfloat16)
    outgoing = (
        jnp.dot(pick_rows, normed, preferred_element_type=jnp.float32)
        .astype(jnp.bfloat16)
        .reshape(experts, 8, capacity * width // 8)
    )
    received = lax.all_to_all(outgoing, EXP, split_axis=0, concat_axis=0, tiled=True)
    gate_full = lax.all_gather(gate_local, "ctx", axis=1, tiled=True)
    up_full = lax.all_gather(up_local, "ctx", axis=1, tiled=True)
    down_full = lax.all_gather(down_local, "ctx", axis=0, tiled=True)
    rows = received.reshape(experts * capacity, width)
    gate = jnp.dot(rows, gate_full, preferred_element_type=jnp.float32)
    upper = jnp.dot(rows, up_full, preferred_element_type=jnp.float32)
    act_all = (jax.nn.silu(gate) * upper).astype(jnp.bfloat16)
    quarter = w_down.shape[1]
    quarter_terms = jnp.einsum(
        "rqf,qfd->qrd",
        act_all.reshape(experts * capacity, ctx_count, quarter),
        down_full.reshape(ctx_count, quarter, width),
        preferred_element_type=jnp.float32,
    ).astype(jnp.bfloat16)
    expert_out = (
        jnp.sum(quarter_terms.astype(jnp.float32), axis=0)
        .astype(jnp.bfloat16)
        .reshape(experts, 8, capacity * width // 8)
    )
    returned = lax.all_to_all(expert_out, EXP, split_axis=0, concat_axis=0, tiled=True)
    weigh_rows = jnp.einsum(
        "pr,pt->tr", position_hot, token_hot * combine.reshape(pair_count)[:, None]
    )
    moe_sum = jnp.dot(
        weigh_rows,
        returned.reshape(experts * capacity, width).astype(jnp.float32),
        precision=lax.Precision.HIGHEST,
    )
    return (stream + moe_sum).astype(jnp.bfloat16)


def solution(mesh):
    in_specs = (
        P("ctx", EXP),
        P("ctx", EXP),
        P("ctx", EXP),
        P(EXP, None),
        P(("ctx", *EXP), None),
        P(),
        P(("ctx", *EXP), None),
        P(("ctx", *EXP), None),
        P(EXP, None, "ctx"),
        P(EXP, None, "ctx"),
        P(EXP, "ctx", None),
    )
    out_specs = P(("ctx", *EXP), None)
    split_mesh = Mesh(mesh.devices.reshape(mesh.devices.shape[0], -1, 2), ("ctx", *EXP))
    return jax.shard_map(
        per_device, mesh=split_mesh, in_specs=in_specs, out_specs=out_specs, check_vma=False
    )
```
